128 devices in a mesh: req: 4 (over z), vocab: 32 (over y, x, core).
Axes of the slice: x: 4, y: 4, z: 4, core: 2. Of those that a mesh axis runs over, the one named last changes fastest.
Arguments:
- hidden: bfloat16 [16, 1536, 2048], P('req', 'vocab'), may hold values from -80 to 80
- norm_gain: float32 [2048], replicated, may hold values from 0.6 to 1.4
- head_weight: bfloat16 [2048, 32000], P(None, 'vocab'), may hold values from -2 to 2
- token_ids: int32 [16, 1536], P('req', 'vocab'), may hold values from 0 to 31999
- lengths: int32 [16], replicated, may hold values from 1 to 1536, 15360 in all
- group_ids: int32 [16], replicated, may hold values from 0 to 3
Outputs:
- logprob: float32 [16, 1536], P('req', 'vocab')
- entropy: float32 [16, 1536], P('req', 'vocab')
- centered: float32 [16], replicated
The draws below stay inside these ranges and needn't reach their ends.
Inputs may be any that keep to these rules, and one draw needn't show every extreme that they name: The lengths sum to 15360; the longest is 1536.
All inputs are finite; a program needn't handle non-finite values.
Results may differ from the reference program's by a relative error of at most 0.00093.
Values may be sent and summed in bfloat16 or wider, within the bound.
No kernel may reach another device: no remote copies, remote signals or barrier semaphores. Data moves between devices by JAX's collectives and lax.ppermute only.
A program may use at most 128 MiB of HBM per device.

```python
import math
import jax
import jax.numpy as jnp
import numpy as np
from jax import lax

D = 2048
V = 32000
GROUPS = 4
REQS = 16
LEN = 1536
LIVE = 15360


def planted_columns(key):
    signs = jnp.where(jax.random.normal(jax.random.fold_in(key, 111), (D, 4), jnp.float32) > 0.0, 1.0, -1.0)
    strength = min(1.9, 160.0 / D) * (0.85 + 0.05 * jnp.arange(4, dtype=jnp.float32))
    first_mag = jax.random.uniform(jax.random.fold_in(key, 112), (D, 4), jnp.float32, 0.9, 1.0)
    second_mag = jax.random.uniform(jax.random.fold_in(key, 113), (D, 4), jnp.float32, 0.9, 1.0)
    even_cols = signs * first_mag * strength[None, :]
    odd_cols = signs * second_mag * strength[None, :] * 0.985
    return (even_cols, odd_cols)


def base_head(key):
    weight = jnp.clip(jax.random.normal(jax.random.fold_in(key, 101), (D, V), jnp.float32), -6.0, 6.0)
    weight = jnp.clip(weight * (3.0 / math.sqrt(D)), -2.0, 2.0)
    even_cols, odd_cols = planted_columns(key)
    planted = jnp.stack([even_cols, odd_cols], axis=2).reshape(D, 8)
    return weight.at[:, 0:8].set(planted)


def draw_head_weight(key, part):
    return base_head(key).astype(jnp.bfloat16)


def draw_hidden(key, part):
    values = jnp.clip(jax.random.normal(jax.random.fold_in(key, 202), (REQS, LEN, D), jnp.float32), -6.0, 6.0)
    even_cols, odd_cols = planted_columns(key)
    aligned = jnp.transpose(even_cols) * 20.0
    values = values.at[:, 0:4, :].set(jnp.broadcast_to(aligned[None, :, :], (REQS, 4, D)))
    return values.astype(jnp.bfloat16)


def with_ends(values, key, smallest, largest):
    shape = values.shape
    spot = [jax.random.randint(jax.random.fold_in(key, axis), (), 0, shape[axis]) for axis in range(len(shape))]
    values = values.at[tuple(spot)].set(smallest)
    longest = shape.index(max(shape))
    spot[longest] = (spot[longest] + 1) % shape[longest]
    return values.at[tuple(spot)].set(largest)


def rank_bounds(count, lean):
    portions = [(1 << 20) // math.isqrt(rank ** lean) + 1 for rank in range(1, count + 1)]
    deviation = 1 + sum(portions) // (1 << 30)
    return np.cumsum(np.array([max(1, weight // deviation) for weight in portions]))


def skewed_ids(own_key, shape, count, slope):
    listing = rank_bounds(count, slope)
    ticket = jax.random.randint(jax.random.fold_in(own_key, 1), shape, 0, int(listing[count - 1]))
    standing = jnp.searchsorted(jnp.asarray(listing, jnp.int32), ticket, side="right")
    return jax.random.permutation(jax.random.fold_in(own_key, 2), count)[standing].astype(jnp.int32)


def length_profile(amount, total, limit, slope):
    loads = [(1 << 20) // math.isqrt(standing ** slope) + 1 for standing in range(2, amount + 1)]
    surplus, holding = total - limit - (amount - 1), [1] * (amount - 1)
    while surplus > 0:
        movable = [i for i in range(amount - 1) if holding[i] < limit]
        whole, budget = sum([loads[i] for i in movable]), surplus
        for i in movable:
            extra = min(limit - holding[i], max(1, budget * loads[i] // whole), surplus)
            holding[i] = holding[i] + extra
            surplus = surplus - extra
    return np.array([limit] + holding)


def ragged(own_key, count, total, bound, skew):
    if count == 2:
        one = jax.random.randint(own_key, (), max(1, total - bound), min(bound, total - 1) + 1)
        return jnp.stack([one, total - one])
    sizes = jnp.asarray(length_profile(count, total, bound, skew), jnp.int32)
    couples = (count - 1) // 2
    donor, taker = sizes[1:1 + 2 * couples:2], sizes[2:2 + 2 * couples:2]
    margin = jnp.minimum(donor - 1, bound - taker)
    moved = jax.random.randint(jax.random.fold_in(own_key, 1), (couples,), 0, 1 << 20) % (margin + 1)
    sizes = sizes.at[1:1 + 2 * couples:2].set(donor - moved).at[2:2 + 2 * couples:2].set(taker + moved)
    return sizes[jax.random.permutation(jax.random.fold_in(own_key, 2), count)]


def setup_inputs(seed: int = 0) -> dict:
    arg_keys = jax.random.split(jax.random.key(seed), 7)
    hidden = draw_hidden(jax.random.fold_in(arg_keys[6], 71), 0)
    norm_gain = jnp.clip(1.0 + 0.08 * jax.random.normal(arg_keys[1], (D,), jnp.float32), 0.6, 1.4)
    head_weight = draw_head_weight(jax.random.fold_in(arg_keys[6], 71), 0)
    token_ids = with_ends(skewed_ids(arg_keys[3], (REQS, LEN), V, 2), jax.random.fold_in(arg_keys[3], 3), 0, V - 1).astype(jnp.int32)
    lengths = ragged(arg_keys[4], REQS, LIVE, LEN, 2).astype(jnp.int32)
    group_ids = with_ends(jax.random.randint(arg_keys[5], (REQS,), 0, GROUPS), jax.random.fold_in(arg_keys[5], 1), 0, GROUPS - 1).astype(jnp.int32)
    return dict(hidden=hidden, norm_gain=norm_gain, head_weight=head_weight, token_ids=token_ids, lengths=lengths, group_ids=group_ids)


norm_eps = 1e-06

def block_stats(block_rows, block_tokens, weight):
    logits = jnp.dot(block_rows, weight, preferred_element_type=jnp.float32)
    row_top = lax.optimization_barrier(jnp.max(logits, axis=1))
    exps = jnp.exp(logits - row_top[:, None])
    exp_total = lax.optimization_barrier(jnp.sum(exps, axis=1))
    moment = lax.optimization_barrier(jnp.sum(exps * logits, axis=1))
    columns = jnp.arange(weight.shape[1], dtype=jnp.int32)
    picked = lax.optimization_barrier(jnp.sum(jnp.where(columns[None, :] == block_tokens[:, None], logits, 0.0), axis=1))
    return (row_top, exp_total, moment, picked)

def reference(hidden, norm_gain, head_weight, token_ids, lengths, group_ids):
    block_len = math.gcd(LEN, 512)

    def one_request(packed):
        rows, tokens = packed
        values = rows.astype(jnp.float32)
        squares = lax.optimization_barrier(jnp.mean(values * values, axis=-1, keepdims=True))
        normed = (values * lax.rsqrt(squares + norm_eps) * norm_gain.astype(jnp.float32)).astype(jnp.bfloat16)

        def one_block(inner):
            return block_stats(inner[0], inner[1], head_weight)
        row_top, exp_total, moment, picked = lax.map(one_block, (normed.reshape(LEN // block_len, block_len, D), tokens.reshape(LEN // block_len, block_len)))
        row_top = row_top.reshape(LEN)
        exp_total = exp_total.reshape(LEN)
        moment = moment.reshape(LEN)
        picked = picked.reshape(LEN)
        log_total = row_top + jnp.log(exp_total)
        return (picked - log_total, log_total - moment / exp_total)
    raw_logprob, raw_entropy = lax.map(one_request, (hidden, token_ids))
    positions = jnp.arange(LEN, dtype=jnp.int32)
    is_live = positions[None, :] < lengths[:, None]
    logprob = jnp.where(is_live, raw_logprob, 0.0)
    entropy = jnp.where(is_live, raw_entropy, 0.0)
    seq_sum = lax.optimization_barrier(jnp.sum(logprob, axis=1))
    same = (group_ids[:, None] == group_ids[None, :]).astype(jnp.float32)
    members = lax.optimization_barrier(jnp.sum(same, axis=1))
    group_mean = lax.optimization_barrier(jnp.sum(same * seq_sum[None, :], axis=1)) / members
    spread = lax.optimization_barrier(jnp.sum(same * (seq_sum[None, :] - group_mean[:, None]) ** 2, axis=1)) / members
    group_std = jnp.maximum(jnp.sqrt(spread), 1.0)
    centered = (seq_sum - group_mean) / group_std
    return (logprob, entropy, centered)
```

```python
import jax
import jax.numpy as jnp
from jax import lax
from jax.sharding import PartitionSpec as P

norm_eps = 1e-06
OFFLOAD_FLOATS = 8192


def slice_stats(rows, tokens, weight, offset):
    row_count = rows.shape[0]
    block_len = min(512, row_count)
    columns = jnp.arange(weight.shape[1], dtype=jnp.int32)
    results = []
    for block_start in range(0, row_count, block_len):
        block_rows = rows[block_start : block_start + block_len]
        local_ids = tokens[block_start : block_start + block_len] - offset
        logits = jnp.dot(block_rows, weight, preferred_element_type=jnp.float32)
        row_top = jnp.max(logits, axis=1)
        exps = jnp.exp(logits - row_top[:, None])
        exp_total = jnp.sum(exps, axis=1)
        moment = jnp.sum(exps * logits, axis=1)
        picked = jnp.sum(jnp.where(columns[None, :] == local_ids[:, None], logits, 0.0), axis=1)
        results.append(jnp.stack([row_top, exp_total, moment, picked]))
    return jnp.concatenate(results, axis=1)


def combine(stats):
    maxima, sums, moments, picked = stats[:, 0], stats[:, 1], stats[:, 2], stats[:, 3]
    row_top = jnp.max(maxima, axis=0)
    rescale = jnp.exp(maxima - row_top[None, :])
    exp_total = jnp.sum(sums * rescale, axis=0)
    moment = jnp.sum(moments * rescale, axis=0)
    token_logit = jnp.sum(picked, axis=0)
    log_total = row_top + jnp.log(exp_total)
    return token_logit - log_total, log_total - moment / exp_total


def padded_gather(x, axis_name):
    n = x.shape[0]
    width = max(n, OFFLOAD_FLOATS)
    padded = jnp.zeros((1, width), jnp.float32).at[0, :n].set(x)
    return lax.all_gather(padded, axis_name, axis=0, tiled=True)[:, :n]


def body(hidden, norm_gain, head_weight, token_ids, lengths, group_ids):
    req_dev, pos_dev, model_width = hidden.shape
    vocab_dev = head_weight.shape[1]
    n_vocab = lax.axis_size("vocab")
    n_req = lax.axis_size("req")
    vocab_index = lax.axis_index("vocab")
    req_index = lax.axis_index("req")
    values = hidden.astype(jnp.float32)
    squares = jnp.mean(values * values, axis=-1, keepdims=True)
    normed = (values * lax.rsqrt(squares + norm_eps) * norm_gain).astype(jnp.bfloat16)
    offset = vocab_index * vocab_dev
    tok = padded_gather(token_ids.astype(jnp.float32).reshape(-1), "vocab")
    all_tokens = tok.reshape(n_vocab, req_dev, pos_dev).transpose(1, 0, 2).reshape(req_dev, n_vocab * pos_dev)
    all_tokens = all_tokens.astype(jnp.int32)
    full_len = all_tokens.shape[1]
    own_lengths = lax.dynamic_slice_in_dim(lengths, req_index * req_dev, req_dev)
    positions = jnp.arange(full_len, dtype=jnp.int32)
    logprobs, entropies, seq_parts = [], [], []
    for k in range(req_dev):
        rows = lax.all_gather(normed[k], "vocab", axis=0, tiled=True)
        part = slice_stats(rows, all_tokens[k], head_weight, offset)
        stats = padded_gather(part.reshape(-1), "vocab").reshape(n_vocab, 4, full_len)
        raw_logprob, raw_entropy = combine(stats)
        is_live = positions < own_lengths[k]
        logprob = jnp.where(is_live, raw_logprob, 0.0)
        entropy = jnp.where(is_live, raw_entropy, 0.0)
        seq_parts.append(jnp.sum(logprob))
        logprobs.append(lax.dynamic_slice_in_dim(logprob, vocab_index * pos_dev, pos_dev))
        entropies.append(lax.dynamic_slice_in_dim(entropy, vocab_index * pos_dev, pos_dev))
    own_seq = jnp.stack(seq_parts)
    slots = jnp.arange(n_req * req_dev, dtype=jnp.int32) // req_dev
    seq_sum = jnp.where(slots == req_index, jnp.tile(own_seq, n_req), 0.0)
    for shift in range(1, n_req):
        moved = lax.ppermute(own_seq, "req", [(i, (i + shift) % n_req) for i in range(n_req)])
        source = (req_index + n_req - shift) % n_req
        seq_sum = seq_sum + jnp.where(slots == source, jnp.tile(moved, n_req), 0.0)
    same = (group_ids[:, None] == group_ids[None, :]).astype(jnp.float32)
    members = jnp.sum(same, axis=1)
    group_mean = jnp.sum(same * seq_sum[None, :], axis=1) / members
    spread = jnp.sum(same * (seq_sum[None, :] - group_mean[:, None]) ** 2, axis=1) / members
    group_std = jnp.maximum(jnp.sqrt(spread), 1.0)
    centered = (seq_sum - group_mean) / group_std
    return (jnp.stack(logprobs), jnp.stack(entropies), centered)


def solution(mesh):
    return jax.shard_map(
        body,
        mesh=mesh,
        in_specs=(P("req", "vocab", None), P(), P(None, "vocab"), P("req", "vocab"), P(), P()),
        out_specs=(P("req", "vocab"), P("req", "vocab"), P()),
        check_vma=False,
    )
```

```python
import jax
import jax.numpy as jnp
from jax import lax
from jax.sharding import PartitionSpec as P

norm_eps = 1e-06

CHIP_CYCLES = (
    (0, 1, 2, 3, 7, 4, 5, 6, 10, 11, 8, 9, 13, 14, 15, 12),
    (0, 3, 15, 11, 7, 6, 2, 14, 10, 9, 5, 1, 13, 12, 8, 4),
)


def device_ring(chips):
    ring = []
    for i, chip in enumerate(chips):
        cores = (0, 1) if i % 2 == 0 else (1, 0)
        ring.extend(2 * chip + core for core in cores)
    return ring


def ring_perms(n):
    if n == 32:
        rings = [device_ring(c) for c in CHIP_CYCLES]
    else:
        rings = [list(range(n)), list(range(n))]
    perms = []
    for ring in rings:
        place = {d: i for i, d in enumerate(ring)}
        for step in (1, -1):
            perms.append([(d, ring[(place[d] + step) % n]) for d in range(n)])
    return perms


def local_stats(rows, tokens, weight, offset):
    logits = jnp.dot(rows, weight, preferred_element_type=jnp.float32)
    row_top = jnp.max(logits, axis=1)
    exps = jnp.exp(logits - row_top[:, None])
    exp_total = jnp.sum(exps, axis=1)
    moment = jnp.sum(exps * logits, axis=1)
    columns = jnp.arange(weight.shape[1], dtype=jnp.int32)
    local_ids = tokens.astype(jnp.int32) - offset
    picked = jnp.sum(jnp.where(columns[None, :] == local_ids[:, None], logits, 0.0), axis=1)
    return row_top, exp_total, moment, picked


def merge(acc, rows, weight, offset):
    flows, _, n = acc.shape
    m1, s1, mo1, p1 = local_stats(rows.reshape(flows * n, -1), acc[:, 4].reshape(-1), weight, offset)
    m1, s1, mo1, p1 = (t.reshape(flows, n) for t in (m1, s1, mo1, p1))
    m0, s0, mo0, p0 = acc[:, 0], acc[:, 1], acc[:, 2], acc[:, 3]
    top = jnp.maximum(m0, m1)
    a = jnp.exp(m0 - top)
    b = jnp.exp(m1 - top)
    return jnp.stack([top, s0 * a + s1 * b, mo0 * a + mo1 * b, p0 + p1, acc[:, 4]], axis=1)


def send(x, perms):
    return jnp.stack([lax.ppermute(x[f], "vocab", perms[f]) for f in range(len(perms))])


def body(hidden, norm_gain, head_weight, token_ids, lengths, group_ids):
    req_dev, pos_dev, model_width = hidden.shape
    vocab_dev = head_weight.shape[1]
    n_vocab = lax.axis_size("vocab")
    n_req = lax.axis_size("req")
    vocab_index = lax.axis_index("vocab")
    req_index = lax.axis_index("req")
    values = hidden.astype(jnp.float32)
    squares = jnp.mean(values * values, axis=-1, keepdims=True)
    normed = (values * lax.rsqrt(squares + norm_eps) * norm_gain).astype(jnp.bfloat16)
    offset = vocab_index * vocab_dev
    perms = ring_perms(n_vocab)
    flows = len(perms)
    assert req_dev == flows
    rows = normed
    tok = token_ids.astype(jnp.float32)
    empty = jnp.zeros((flows, pos_dev), jnp.float32)
    acc = jnp.stack([jnp.full((flows, pos_dev), -jnp.inf, jnp.float32), empty, empty, empty, tok], axis=1)

    def step(_, carry):
        rows, acc = carry
        rows_next = send(rows, perms)
        acc = merge(acc, rows, head_weight, offset)
        return rows_next, send(acc, perms)

    rows, acc = lax.fori_loop(0, n_vocab - 1, step, (rows, acc))
    acc = send(merge(acc, rows, head_weight, offset), perms)
    row_top, exp_total, moment, token_logit = acc[:, 0], acc[:, 1], acc[:, 2], acc[:, 3]
    log_total = row_top + jnp.log(exp_total)
    raw_logprob = token_logit - log_total
    raw_entropy = log_total - moment / exp_total
    positions = vocab_index * pos_dev + jnp.arange(pos_dev, dtype=jnp.int32)
    own_lengths = lax.dynamic_slice_in_dim(lengths, req_index * req_dev, req_dev)
    is_live = positions[None, :] < own_lengths[:, None]
    logprob = jnp.where(is_live, raw_logprob, 0.0)
    entropy = jnp.where(is_live, raw_entropy, 0.0)
    partial_sums = jnp.sum(logprob, axis=1)
    request_count = lengths.shape[0]
    slots = jnp.arange(request_count, dtype=jnp.int32)
    global_rows = req_index * req_dev + jnp.arange(req_dev, dtype=jnp.int32)
    seq_sum = jnp.sum(jnp.where(slots[None, :] == global_rows[:, None], partial_sums[:, None], 0.0), axis=0)
    for axis, size in (("vocab", n_vocab), ("req", n_req)):
        bit = 1
        while bit < size:
            seq_sum = seq_sum + lax.ppermute(seq_sum, axis, [(i, i ^ bit) for i in range(size)])
            bit *= 2
    same = (group_ids[:, None] == group_ids[None, :]).astype(jnp.float32)
    members = jnp.sum(same, axis=1)
    group_mean = jnp.sum(same * seq_sum[None, :], axis=1) / members
    spread = jnp.sum(same * (seq_sum[None, :] - group_mean[:, None]) ** 2, axis=1) / members
    group_std = jnp.maximum(jnp.sqrt(spread), 1.0)
    centered = (seq_sum - group_mean) / group_std
    return (logprob, entropy, centered)


def solution(mesh):
    return jax.shard_map(
        body,
        mesh=mesh,
        in_specs=(P("req", "vocab", None), P(), P(None, "vocab"), P("req", "vocab"), P(), P()),
        out_specs=(P("req", "vocab"), P("req", "vocab"), P()),
        check_vma=False,
    )
```

```python
import jax
import jax.numpy as jnp
from jax import lax
from jax.sharding import PartitionSpec as P

norm_eps = 1e-06
BLOCK = 512


def block_stats(rows, tokens, weight, offset):
    logits = jnp.dot(rows, weight, preferred_element_type=jnp.float32)
    row_top = jnp.max(logits, axis=1)
    exps = jnp.exp(logits - row_top[:, None])
    exp_total = jnp.sum(exps, axis=1)
    moment = jnp.sum(exps * logits, axis=1)
    columns = jnp.arange(weight.shape[1], dtype=jnp.int32)
    picked = jnp.sum(jnp.where(columns[None, :] == (tokens - offset)[:, None], logits, 0.0), axis=1)
    return jnp.stack([row_top, exp_total, moment, picked])


def idle_stats(n):
    zero = jnp.zeros((n,), jnp.float32)
    return jnp.stack([zero, zero + 1.0, zero, zero])


def merge(a, b):
    top = jnp.maximum(a[0], b[0])
    ea = jnp.exp(a[0] - top)
    eb = jnp.exp(b[0] - top)
    return jnp.stack([top, a[1] * ea + b[1] * eb, a[2] * ea + b[2] * eb, a[3] + b[3]])


def xor_gather(x, axis, size, index):
    bit = 1
    while bit < size:
        other = lax.ppermute(x, axis, [(i, i ^ bit) for i in range(size)])
        upper = (index & bit) != 0
        x = jnp.concatenate([jnp.where(upper, other, x), jnp.where(upper, x, other)], axis=0)
        bit *= 2
    return x


def xor_reduce(x, axis, size, combine):
    bit = 1
    while bit < size:
        x = combine(x, lax.ppermute(x, axis, [(i, i ^ bit) for i in range(size)]))
        bit *= 2
    return x


def body(hidden, norm_gain, head_weight, token_ids, lengths, group_ids):
    req_dev, pos_dev, model_width = hidden.shape
    vocab_dev = head_weight.shape[1]
    n_vocab = lax.axis_size("vocab")
    n_req = lax.axis_size("req")
    vocab_index = lax.axis_index("vocab")
    req_index = lax.axis_index("req")
    values = hidden.astype(jnp.float32)
    squares = jnp.mean(values * values, axis=-1, keepdims=True)
    normed = (values * lax.rsqrt(squares + norm_eps) * norm_gain).astype(jnp.bfloat16)
    offset = vocab_index * vocab_dev
    rows = lax.all_gather(normed, "vocab", axis=1, tiled=True)
    full_len = rows.shape[1]
    tokens = xor_gather(token_ids.T, "vocab", n_vocab, vocab_index)
    own_lengths = lax.dynamic_slice_in_dim(lengths, req_index * req_dev, req_dev)
    per_request = []
    for k in range(req_dev):
        blocks = []
        for start in range(0, full_len, BLOCK):
            size = min(BLOCK, full_len - start)
            blocks.append(
                lax.cond(
                    start < own_lengths[k],
                    lambda r, t: block_stats(r, t, head_weight, offset),
                    lambda r, t: idle_stats(r.shape[0]),
                    rows[k, start : start + size],
                    tokens[start : start + size, k],
                )
            )
        per_request.append(jnp.concatenate(blocks, axis=1))
    stats = jnp.stack(per_request, axis=1)
    stats = xor_reduce(stats, "vocab", n_vocab, merge)
    row_top, exp_total, moment, token_logit = stats[0], stats[1], stats[2], stats[3]
    log_total = row_top + jnp.log(exp_total)
    raw_logprob = token_logit - log_total
    raw_entropy = log_total - moment / exp_total
    positions = jnp.arange(full_len, dtype=jnp.int32)
    is_live = positions[None, :] < own_lengths[:, None]
    logprob = jnp.where(is_live, raw_logprob, 0.0)
    entropy = jnp.where(is_live, raw_entropy, 0.0)
    own_seq = jnp.sum(logprob, axis=1)
    request_count = lengths.shape[0]
    slots = jnp.arange(request_count, dtype=jnp.int32)
    global_rows = req_index * req_dev + jnp.arange(req_dev, dtype=jnp.int32)
    seq_sum = jnp.sum(jnp.where(slots[None, :] == global_rows[:, None], own_seq[:, None], 0.0), axis=0)
    seq_sum = xor_reduce(seq_sum, "req", n_req, jnp.add)
    same = (group_ids[:, None] == group_ids[None, :]).astype(jnp.float32)
    members = jnp.sum(same, axis=1)
    group_mean = jnp.sum(same * seq_sum[None, :], axis=1) / members
    spread = jnp.sum(same * (seq_sum[None, :] - group_mean[:, None]) ** 2, axis=1) / members
    group_std = jnp.maximum(jnp.sqrt(spread), 1.0)
    centered = (seq_sum - group_mean) / group_std
    own = vocab_index * pos_dev
    return (
        lax.dynamic_slice_in_dim(logprob, own, pos_dev, axis=1),
        lax.dynamic_slice_in_dim(entropy, own, pos_dev, axis=1),
        centered,
    )


def solution(mesh):
    return jax.shard_map(
        body,
        mesh=mesh,
        in_specs=(P("req", "vocab", None), P(), P(None, "vocab"), P("req", "vocab"), P(), P()),
        out_specs=(P("req", "vocab"), P("req", "vocab"), P()),
        check_vma=False,
    )
```

```python
import jax
import jax.numpy as jnp
from jax import lax
from jax.sharding import PartitionSpec as P

norm_eps = 1e-06
BLOCK = 512


def block_stats(rows, tokens, weight, offset):
    logits = jnp.dot(rows, weight, preferred_element_type=jnp.float32)
    row_top = jnp.max(logits, axis=1)
    exps = jnp.exp(logits - row_top[:, None])
    exp_total = jnp.sum(exps, axis=1)
    moment = jnp.sum(exps * logits, axis=1)
    columns = jnp.arange(weight.shape[1], dtype=jnp.int32)
    picked = jnp.sum(jnp.where(columns[None, :] == (tokens - offset)[:, None], logits, 0.0), axis=1)
    return jnp.stack([row_top, exp_total, moment, picked])


def idle_stats(n):
    zero = jnp.zeros((n,), jnp.float32)
    return jnp.stack([zero, zero + 1.0, zero, zero])


def merge(a, b):
    top = jnp.maximum(a[0], b[0])
    ea = jnp.exp(a[0] - top)
    eb = jnp.exp(b[0] - top)
    return jnp.stack([top, a[1] * ea + b[1] * eb, a[2] * ea + b[2] * eb, a[3] + b[3]])


def xor_gather(x, axis, size, index):
    bit = 1
    while bit < size:
        other = lax.ppermute(x, axis, [(i, i ^ bit) for i in range(size)])
        upper = (index & bit) != 0
        x = jnp.concatenate([jnp.where(upper, other, x), jnp.where(upper, x, other)], axis=0)
        bit *= 2
    return x


def xor_reduce(x, axis, size, combine):
    bit = 1
    while bit < size:
        x = combine(x, lax.ppermute(x, axis, [(i, i ^ bit) for i in range(size)]))
        bit *= 2
    return x


def body(hidden, norm_gain, head_weight, token_ids, lengths, group_ids):
    req_dev, pos_dev, model_width = hidden.shape
    vocab_dev = head_weight.shape[1]
    n_vocab = lax.axis_size("vocab")
    n_req = lax.axis_size("req")
    vocab_index = lax.axis_index("vocab")
    req_index = lax.axis_index("req")
    values = hidden.astype(jnp.float32)
    squares = jnp.mean(values * values, axis=-1, keepdims=True)
    normed = (values * lax.rsqrt(squares + norm_eps) * norm_gain).astype(jnp.bfloat16)
    offset = vocab_index * vocab_dev
    rows = lax.all_gather(normed, "vocab", axis=1, tiled=True)
    full_len = rows.shape[1]
    tokens = xor_gather(token_ids.T, "vocab", n_vocab, vocab_index)
    own_lengths = lax.dynamic_slice_in_dim(lengths, req_index * req_dev, req_dev)
    per_request = []
    for k in range(req_dev):
        blocks = []
        for start in range(0, full_len, BLOCK):
            size = min(BLOCK, full_len - start)
            blocks.append(
                lax.cond(
                    start < own_lengths[k],
                    lambda r, t: block_stats(r, t, head_weight, offset),
                    lambda r, t: idle_stats(r.shape[0]),
                    rows[k, start : start + size],
                    tokens[start : start + size, k],
                )
            )
        per_request.append(xor_reduce(jnp.concatenate(blocks, axis=1), "vocab", n_vocab, merge))
    stats = jnp.stack(per_request, axis=1)
    row_top, exp_total, moment, token_logit = stats[0], stats[1], stats[2], stats[3]
    log_total = row_top + jnp.log(exp_total)
    raw_logprob = token_logit - log_total
    raw_entropy = log_total - moment / exp_total
    positions = jnp.arange(full_len, dtype=jnp.int32)
    is_live = positions[None, :] < own_lengths[:, None]
    logprob = jnp.where(is_live, raw_logprob, 0.0)
    entropy = jnp.where(is_live, raw_entropy, 0.0)
    own_seq = jnp.sum(logprob, axis=1)
    request_count = lengths.shape[0]
    slots = jnp.arange(request_count, dtype=jnp.int32)
    global_rows = req_index * req_dev + jnp.arange(req_dev, dtype=jnp.int32)
    seq_sum = jnp.sum(jnp.where(slots[None, :] == global_rows[:, None], own_seq[:, None], 0.0), axis=0)
    seq_sum = xor_reduce(seq_sum, "req", n_req, jnp.add)
    same = (group_ids[:, None] == group_ids[None, :]).astype(jnp.float32)
    members = jnp.sum(same, axis=1)
    group_mean = jnp.sum(same * seq_sum[None, :], axis=1) / members
    spread = jnp.sum(same * (seq_sum[None, :] - group_mean[:, None]) ** 2, axis=1) / members
    group_std = jnp.maximum(jnp.sqrt(spread), 1.0)
    centered = (seq_sum - group_mean) / group_std
    own = vocab_index * pos_dev
    return (
        lax.dynamic_slice_in_dim(logprob, own, pos_dev, axis=1),
        lax.dynamic_slice_in_dim(entropy, own, pos_dev, axis=1),
        centered,
    )


def solution(mesh):
    return jax.shard_map(
        body,
        mesh=mesh,
        in_specs=(P("req", "vocab", None), P(), P(None, "vocab"), P("req", "vocab"), P(), P()),
        out_specs=(P("req", "vocab"), P("req", "vocab"), P()),
        check_vma=False,
    )
```

```python
import jax
import jax.numpy as jnp
from jax import lax
from jax.sharding import PartitionSpec as P

norm_eps = 1e-06
BLOCK = 512


def block_stats(rows, tokens, weight, offset):
    logits = jnp.dot(rows, weight, preferred_element_type=jnp.float32)
    row_top = jnp.max(logits, axis=1)
    exps = jnp.exp(logits - row_top[:, None])
    exp_total = jnp.sum(exps, axis=1)
    moment = jnp.sum(exps * logits, axis=1)
    columns = jnp.arange(weight.shape[1], dtype=jnp.int32)
    picked = jnp.sum(jnp.where(columns[None, :] == (tokens - offset)[:, None], logits, 0.0), axis=1)
    return jnp.stack([row_top, exp_total, moment, picked])


def idle_stats(n):
    zero = jnp.zeros((n,), jnp.float32)
    return jnp.stack([zero, zero + 1.0, zero, zero])


def merge(a, b):
    top = jnp.maximum(a[0], b[0])
    ea = jnp.exp(a[0] - top)
    eb = jnp.exp(b[0] - top)
    return jnp.stack([top, a[1] * ea + b[1] * eb, a[2] * ea + b[2] * eb, a[3] + b[3]])


def xor_gather(x, axis, size, index):
    bit = 1
    while bit < size:
        other = lax.ppermute(x, axis, [(i, i ^ bit) for i in range(size)])
        upper = (index & bit) != 0
        x = jnp.concatenate([jnp.where(upper, other, x), jnp.where(upper, x, other)], axis=0)
        bit *= 2
    return x


def xor_reduce(x, axis, size, combine):
    bit = 1
    while bit < size:
        x = combine(x, lax.ppermute(x, axis, [(i, i ^ bit) for i in range(size)]))
        bit *= 2
    return x


def body(hidden, norm_gain, head_weight, token_ids, lengths, group_ids):
    req_dev, pos_dev, model_width = hidden.shape
    vocab_dev = head_weight.shape[1]
    n_vocab = lax.axis_size("vocab")
    n_req = lax.axis_size("req")
    vocab_index = lax.axis_index("vocab")
    req_index = lax.axis_index("req")
    values = hidden.astype(jnp.float32)
    squares = jnp.mean(values * values, axis=-1, keepdims=True)
    normed = (values * lax.rsqrt(squares + norm_eps) * norm_gain).astype(jnp.bfloat16)
    offset = vocab_index * vocab_dev
    rows = lax.all_gather(normed, "vocab", axis=1, tiled=True)
    full_len = rows.shape[1]
    tokens = xor_gather(token_ids.T, "vocab", n_vocab, vocab_index)
    own_lengths = lax.dynamic_slice_in_dim(lengths, req_index * req_dev, req_dev)
    per_request = []
    for k in range(req_dev):
        blocks = []
        for start in range(0, full_len, BLOCK):
            size = min(BLOCK, full_len - start)
            blocks.append(block_stats(rows[k, start : start + size], tokens[start : start + size, k], head_weight, offset))
        per_request.append(xor_reduce(jnp.concatenate(blocks, axis=1), "vocab", n_vocab, merge))
    stats = jnp.stack(per_request, axis=1)
    row_top, exp_total, moment, token_logit = stats[0], stats[1], stats[2], stats[3]
    log_total = row_top + jnp.log(exp_total)
    raw_logprob = token_logit - log_total
    raw_entropy = log_total - moment / exp_total
    positions = jnp.arange(full_len, dtype=jnp.int32)
    is_live = positions[None, :] < own_lengths[:, None]
    logprob = jnp.where(is_live, raw_logprob, 0.0)
    entropy = jnp.where(is_live, raw_entropy, 0.0)
    own_seq = jnp.sum(logprob, axis=1)
    request_count = lengths.shape[0]
    slots = jnp.arange(request_count, dtype=jnp.int32)
    global_rows = req_index * req_dev + jnp.arange(req_dev, dtype=jnp.int32)
    seq_sum = jnp.sum(jnp.where(slots[None, :] == global_rows[:, None], own_seq[:, None], 0.0), axis=0)
    seq_sum = xor_reduce(seq_sum, "req", n_req, jnp.add)
    same = (group_ids[:, None] == group_ids[None, :]).astype(jnp.float32)
    members = jnp.sum(same, axis=1)
    group_mean = jnp.sum(same * seq_sum[None, :], axis=1) / members
    spread = jnp.sum(same * (seq_sum[None, :] - group_mean[:, None]) ** 2, axis=1) / members
    group_std = jnp.maximum(jnp.sqrt(spread), 1.0)
    centered = (seq_sum - group_mean) / group_std
    own = vocab_index * pos_dev
    return (
        lax.dynamic_slice_in_dim(logprob, own, pos_dev, axis=1),
        lax.dynamic_slice_in_dim(entropy, own, pos_dev, axis=1),
        centered,
    )


def solution(mesh):
    return jax.shard_map(
        body,
        mesh=mesh,
        in_specs=(P("req", "vocab", None), P(), P(None, "vocab"), P("req", "vocab"), P(), P()),
        out_specs=(P("req", "vocab"), P("req", "vocab"), P()),
        check_vma=False,
    )
```

```python
import jax
import jax.numpy as jnp
from jax import lax
from jax.sharding import PartitionSpec as P

norm_eps = 1e-06
BLOCK = 512


def block_stats(rows, tokens, weight, offset):
    logits = jnp.dot(rows, weight, preferred_element_type=jnp.float32)
    row_top = jnp.max(logits, axis=1)
    exps = jnp.exp(logits - row_top[:, None])
    exp_total = jnp.sum(exps, axis=1)
    moment = jnp.sum(exps * logits, axis=1)
    columns = jnp.arange(weight.shape[1], dtype=jnp.int32)
    picked = jnp.sum(jnp.where(columns[None, :] == (tokens - offset)[:, None], logits, 0.0), axis=1)
    return jnp.stack([row_top, exp_total, moment, picked])


def merge(a, b):
    top = jnp.maximum(a[0], b[0])
    ea = jnp.exp(a[0] - top)
    eb = jnp.exp(b[0] - top)
    return jnp.stack([top, a[1] * ea + b[1] * eb, a[2] * ea + b[2] * eb, a[3] + b[3]])


def xor_gather(x, axis, size, index):
    bit = 1
    while bit < size:
        other = lax.ppermute(x, axis, [(i, i ^ bit) for i in range(size)])
        upper = (index & bit) != 0
        x = jnp.concatenate([jnp.where(upper, other, x), jnp.where(upper, x, other)], axis=0)
        bit *= 2
    return x


def group_reduce(x, axis, size, index, combine):
    bit = 1
    while bit < size:
        bits = [b for b in (bit, 2 * bit) if b < size]
        offsets = [0, bits[0]] if len(bits) == 1 else [0, bits[0], bits[1], bits[0] | bits[1]]
        got = [x] + [lax.ppermute(x, axis, [(i, i ^ d) for i in range(size)]) for d in offsets[1:]]
        stacked = jnp.stack(got)
        own = index & sum(bits)
        ordered = []
        for m in offsets:
            d = own ^ m
            place = (d & bits[0]) // bits[0]
            if len(bits) == 2:
                place = place + 2 * ((d & bits[1]) // bits[1])
            ordered.append(lax.dynamic_index_in_dim(stacked, place, keepdims=False))
        while len(ordered) > 1:
            ordered = [combine(ordered[i], ordered[i + 1]) for i in range(0, len(ordered), 2)]
        x = ordered[0]
        bit *= 2 ** len(bits)
    return x


def body(hidden, norm_gain, head_weight, token_ids, lengths, group_ids):
    req_dev, pos_dev, model_width = hidden.shape
    vocab_dev = head_weight.shape[1]
    n_vocab = lax.axis_size("vocab")
    n_req = lax.axis_size("req")
    vocab_index = lax.axis_index("vocab")
    req_index = lax.axis_index("req")
    values = hidden.astype(jnp.float32)
    squares = jnp.mean(values * values, axis=-1, keepdims=True)
    normed = (values * lax.rsqrt(squares + norm_eps) * norm_gain).astype(jnp.bfloat16)
    offset = vocab_index * vocab_dev
    rows = lax.all_gather(normed, "vocab", axis=1, tiled=True)
    full_len = rows.shape[1]
    tokens = xor_gather(token_ids.T, "vocab", n_vocab, vocab_index)
    own_lengths = lax.dynamic_slice_in_dim(lengths, req_index * req_dev, req_dev)
    per_request = []
    for k in range(req_dev):
        blocks = []
        for start in range(0, full_len, BLOCK):
            size = min(BLOCK, full_len - start)
            blocks.append(block_stats(rows[k, start : start + size], tokens[start : start + size, k], head_weight, offset))
        per_request.append(group_reduce(jnp.concatenate(blocks, axis=1), "vocab", n_vocab, vocab_index, merge))
    stats = jnp.stack(per_request, axis=1)
    row_top, exp_total, moment, token_logit = stats[0], stats[1], stats[2], stats[3]
    log_total = row_top + jnp.log(exp_total)
    raw_logprob = token_logit - log_total
    raw_entropy = log_total - moment / exp_total
    positions = jnp.arange(full_len, dtype=jnp.int32)
    is_live = positions[None, :] < own_lengths[:, None]
    logprob = jnp.where(is_live, raw_logprob, 0.0)
    entropy = jnp.where(is_live, raw_entropy, 0.0)
    own_seq = jnp.sum(logprob, axis=1)
    request_count = lengths.shape[0]
    slots = jnp.arange(request_count, dtype=jnp.int32)
    global_rows = req_index * req_dev + jnp.arange(req_dev, dtype=jnp.int32)
    seq_sum = jnp.sum(jnp.where(slots[None, :] == global_rows[:, None], own_seq[:, None], 0.0), axis=0)
    seq_sum = group_reduce(seq_sum, "req", n_req, req_index, jnp.add)
    same = (group_ids[:, None] == group_ids[None, :]).astype(jnp.float32)
    members = jnp.sum(same, axis=1)
    group_mean = jnp.sum(same * seq_sum[None, :], axis=1) / members
    spread = jnp.sum(same * (seq_sum[None, :] - group_mean[:, None]) ** 2, axis=1) / members
    group_std = jnp.maximum(jnp.sqrt(spread), 1.0)
    centered = (seq_sum - group_mean) / group_std
    own = vocab_index * pos_dev
    return (
        lax.dynamic_slice_in_dim(logprob, own, pos_dev, axis=1),
        lax.dynamic_slice_in_dim(entropy, own, pos_dev, axis=1),
        centered,
    )


def solution(mesh):
    return jax.shard_map(
        body,
        mesh=mesh,
        in_specs=(P("req", "vocab", None), P(), P(None, "vocab"), P("req", "vocab"), P(), P()),
        out_specs=(P("req", "vocab"), P("req", "vocab"), P()),
        check_vma=False,
    )
```

```python
import jax
import jax.numpy as jnp
import numpy as np
from jax import lax
from jax.sharding import Mesh
from jax.sharding import PartitionSpec as P

norm_eps = 1e-06
BLOCK = 384


def block_stats(rows, tokens, weight, offset):
    logits = jnp.dot(rows, weight, preferred_element_type=jnp.float32)
    row_top = jnp.max(logits, axis=1)
    exps = jnp.exp(logits - row_top[:, None])
    exp_total = jnp.sum(exps, axis=1)
    moment = jnp.sum(exps * logits, axis=1)
    columns = jnp.arange(weight.shape[1], dtype=jnp.int32)
    picked = jnp.sum(jnp.where(columns[None, :] == (tokens - offset)[:, None], logits, 0.0), axis=1)
    return jnp.stack([row_top, exp_total, moment, picked])


def merge(a, b):
    top = jnp.maximum(a[0], b[0])
    ea = jnp.exp(a[0] - top)
    eb = jnp.exp(b[0] - top)
    return jnp.stack([top, a[1] * ea + b[1] * eb, a[2] * ea + b[2] * eb, a[3] + b[3]])


def xor_gather(x, axis, size, index):
    bit = 1
    while bit < size:
        other = lax.ppermute(x, axis, [(i, i ^ bit) for i in range(size)])
        upper = (index & bit) != 0
        x = jnp.concatenate([jnp.where(upper, other, x), jnp.where(upper, x, other)], axis=0)
        bit *= 2
    return x


def xor_reduce(x, axis, size, combine):
    bit = 1
    while bit < size:
        x = combine(x, lax.ppermute(x, axis, [(i, i ^ bit) for i in range(size)]))
        bit *= 2
    return x


def body(hidden, norm_gain, head_weight, token_ids, lengths, group_ids):
    req_dev, pos_dev, model_width = hidden.shape
    vocab_dev = head_weight.shape[1]
    n_chip = lax.axis_size("chip")
    n_core = lax.axis_size("core")
    n_req = lax.axis_size("req")
    chip = lax.axis_index("chip")
    core = lax.axis_index("core")
    req_index = lax.axis_index("req")
    values = hidden.astype(jnp.float32)
    squares = jnp.mean(values * values, axis=-1, keepdims=True)
    normed = (values * lax.rsqrt(squares + norm_eps) * norm_gain).astype(jnp.bfloat16)
    rows = lax.all_gather(normed, "chip", axis=1, tiled=True)
    other = lax.ppermute(head_weight, "core", [(0, 1), (1, 0)])
    first = core == 0
    weight = jnp.concatenate([jnp.where(first, head_weight, other), jnp.where(first, other, head_weight)], axis=1)
    offset = chip * (n_core * vocab_dev)
    half_len = rows.shape[1]
    tokens = xor_gather(token_ids.T, "chip", n_chip, chip)
    own_lengths = lax.dynamic_slice_in_dim(lengths, req_index * req_dev, req_dev)
    per_request = []
    for k in range(req_dev):
        blocks = []
        for start in range(0, half_len, BLOCK):
            size = min(BLOCK, half_len - start)
            blocks.append(block_stats(rows[k, start : start + size], tokens[start : start + size, k], weight, offset))
        per_request.append(jnp.concatenate(blocks, axis=1))
    stats = jnp.stack(per_request, axis=1)
    stats = xor_reduce(stats, "chip", n_chip, merge)
    row_top, exp_total, moment, token_logit = stats[0], stats[1], stats[2], stats[3]
    log_total = row_top + jnp.log(exp_total)
    raw_logprob = token_logit - log_total
    raw_entropy = log_total - moment / exp_total
    index = jnp.arange(half_len, dtype=jnp.int32)
    positions = ((index // pos_dev) * n_core + core) * pos_dev + index % pos_dev
    is_live = positions[None, :] < own_lengths[:, None]
    logprob = jnp.where(is_live, raw_logprob, 0.0)
    entropy = jnp.where(is_live, raw_entropy, 0.0)
    half_seq = jnp.sum(logprob, axis=1)
    own_seq = half_seq + lax.ppermute(half_seq, "core", [(0, 1), (1, 0)])
    request_count = lengths.shape[0]
    slots = jnp.arange(request_count, dtype=jnp.int32)
    global_rows = req_index * req_dev + jnp.arange(req_dev, dtype=jnp.int32)
    seq_sum = jnp.sum(jnp.where(slots[None, :] == global_rows[:, None], own_seq[:, None], 0.0), axis=0)
    seq_sum = xor_reduce(seq_sum, "req", n_req, jnp.add)
    same = (group_ids[:, None] == group_ids[None, :]).astype(jnp.float32)
    members = jnp.sum(same, axis=1)
    group_mean = jnp.sum(same * seq_sum[None, :], axis=1) / members
    spread = jnp.sum(same * (seq_sum[None, :] - group_mean[:, None]) ** 2, axis=1) / members
    group_std = jnp.maximum(jnp.sqrt(spread), 1.0)
    centered = (seq_sum - group_mean) / group_std
    own = chip * pos_dev
    return (
        lax.dynamic_slice_in_dim(logprob, own, pos_dev, axis=1),
        lax.dynamic_slice_in_dim(entropy, own, pos_dev, axis=1),
        centered,
    )


def solution(mesh):
    n_req, n_vocab = mesh.devices.shape
    split = Mesh(np.asarray(mesh.devices).reshape(n_req, n_vocab // 2, 2), ("req", "chip", "core"))
    vocab = ("chip", "core")
    return jax.shard_map(
        body,
        mesh=split,
        in_specs=(P("req", vocab, None), P(), P(None, vocab), P("req", vocab), P(), P()),
        out_specs=(P("req", vocab), P("req", vocab), P()),
        check_vma=False,
    )
```

```python
import functools

import jax
import jax.numpy as jnp
import numpy as np
from jax import lax
from jax.sharding import Mesh
from jax.sharding import PartitionSpec as P

norm_eps = 1e-06
BLOCK = 384


def block_stats(rows, tokens, weights, offsets):
    logits = [jnp.dot(rows, w, preferred_element_type=jnp.float32) for w in weights]
    row_top = functools.reduce(jnp.maximum, [jnp.max(l, axis=1) for l in logits])
    exp_total, moment, picked = 0.0, 0.0, 0.0
    for l, w, o in zip(logits, weights, offsets):
        exps = jnp.exp(l - row_top[:, None])
        exp_total = exp_total + jnp.sum(exps, axis=1)
        moment = moment + jnp.sum(exps * l, axis=1)
        columns = jnp.arange(w.shape[1], dtype=jnp.int32)
        picked = picked + jnp.sum(jnp.where(columns[None, :] == (tokens - o)[:, None], l, 0.0), axis=1)
    return jnp.stack([row_top, exp_total, moment, picked])


def merge(a, b):
    top = jnp.maximum(a[0], b[0])
    ea = jnp.exp(a[0] - top)
    eb = jnp.exp(b[0] - top)
    return jnp.stack([top, a[1] * ea + b[1] * eb, a[2] * ea + b[2] * eb, a[3] + b[3]])


def xor_gather(x, axis, size, index):
    bit = 1
    while bit < size:
        other = lax.ppermute(x, axis, [(i, i ^ bit) for i in range(size)])
        upper = (index & bit) != 0
        x = jnp.concatenate([jnp.where(upper, other, x), jnp.where(upper, x, other)], axis=0)
        bit *= 2
    return x


def xor_reduce(x, axis, size, combine):
    bit = 1
    while bit < size:
        x = combine(x, lax.ppermute(x, axis, [(i, i ^ bit) for i in range(size)]))
        bit *= 2
    return x


def body(hidden, norm_gain, head_weight, token_ids, lengths, group_ids):
    req_dev, pos_dev, model_width = hidden.shape
    vocab_dev = head_weight.shape[1]
    chips = ("y", "x")
    n_chip = lax.axis_size(chips)
    n_core = lax.axis_size("core")
    n_req = lax.axis_size("req")
    chip = lax.axis_index(chips)
    core = lax.axis_index("core")
    req_index = lax.axis_index("req")
    values = hidden.astype(jnp.float32)
    squares = jnp.mean(values * values, axis=-1, keepdims=True)
    normed = (values * lax.rsqrt(squares + norm_eps) * norm_gain).astype(jnp.bfloat16)
    rows = lax.all_gather(normed, "x", axis=1, tiled=True)
    rows = lax.all_gather(rows, "y", axis=1, tiled=True)
    other = lax.ppermute(head_weight, "core", [(0, 1), (1, 0)])
    weights = (head_weight, other)
    offsets = ((chip * n_core + core) * vocab_dev, (chip * n_core + (1 - core)) * vocab_dev)
    half_len = rows.shape[1]
    tokens = xor_gather(token_ids.T, chips, n_chip, chip)
    own_lengths = lax.dynamic_slice_in_dim(lengths, req_index * req_dev, req_dev)
    per_request = []
    for k in range(req_dev):
        blocks = []
        for start in range(0, half_len, BLOCK):
            size = min(BLOCK, half_len - start)
            blocks.append(block_stats(rows[k, start : start + size], tokens[start : start + size, k], weights, offsets))
        per_request.append(jnp.concatenate(blocks, axis=1))
    stats = jnp.stack(per_request, axis=1)
    stats = xor_reduce(stats, chips, n_chip, merge)
    row_top, exp_total, moment, token_logit = stats[0], stats[1], stats[2], stats[3]
    log_total = row_top + jnp.log(exp_total)
    raw_logprob = token_logit - log_total
    raw_entropy = log_total - moment / exp_total
    index = jnp.arange(half_len, dtype=jnp.int32)
    positions = ((index // pos_dev) * n_core + core) * pos_dev + index % pos_dev
    is_live = positions[None, :] < own_lengths[:, None]
    logprob = jnp.where(is_live, raw_logprob, 0.0)
    entropy = jnp.where(is_live, raw_entropy, 0.0)
    half_seq = jnp.sum(logprob, axis=1)
    own_seq = half_seq + lax.ppermute(half_seq, "core", [(0, 1), (1, 0)])
    request_count = lengths.shape[0]
    slots = jnp.arange(request_count, dtype=jnp.int32)
    global_rows = req_index * req_dev + jnp.arange(req_dev, dtype=jnp.int32)
    seq_sum = jnp.sum(jnp.where(slots[None, :] == global_rows[:, None], own_seq[:, None], 0.0), axis=0)
    seq_sum = xor_reduce(seq_sum, "req", n_req, jnp.add)
    same = (group_ids[:, None] == group_ids[None, :]).astype(jnp.float32)
    members = jnp.sum(same, axis=1)
    group_mean = jnp.sum(same * seq_sum[None, :], axis=1) / members
    spread = jnp.sum(same * (seq_sum[None, :] - group_mean[:, None]) ** 2, axis=1) / members
    group_std = jnp.maximum(jnp.sqrt(spread), 1.0)
    centered = (seq_sum - group_mean) / group_std
    own = chip * pos_dev
    return (
        lax.dynamic_slice_in_dim(logprob, own, pos_dev, axis=1),
        lax.dynamic_slice_in_dim(entropy, own, pos_dev, axis=1),
        centered,
    )


def solution(mesh):
    n_req, n_vocab = mesh.devices.shape
    side = int(round((n_vocab // 2) ** 0.5))
    split = Mesh(np.asarray(mesh.devices).reshape(n_req, side, n_vocab // 2 // side, 2), ("req", "y", "x", "core"))
    vocab = ("y", "x", "core")
    return jax.shard_map(
        body,
        mesh=split,
        in_specs=(P("req", vocab, None), P(), P(None, vocab), P("req", vocab), P(), P()),
        out_specs=(P("req", vocab), P("req", vocab), P()),
        check_vma=False,
    )
```

```python
import jax
import jax.numpy as jnp
import numpy as np
from jax import lax
from jax.sharding import Mesh
from jax.sharding import PartitionSpec as P

norm_eps = 1e-06
BLOCK = 768


def block_stats(rows, tokens, weight, offset):
    logits = jnp.dot(rows, weight, preferred_element_type=jnp.float32)
    row_top = jnp.max(logits, axis=1)
    exps = jnp.exp(logits - row_top[:, None])
    exp_total = jnp.sum(exps, axis=1)
    moment = jnp.sum(exps * logits, axis=1)
    columns = jnp.arange(weight.shape[1], dtype=jnp.int32)
    picked = jnp.sum(jnp.where(columns[None, :] == (tokens - offset)[:, None], logits, 0.0), axis=1)
    return jnp.stack([row_top, exp_total, moment, picked])


def merge(a, b):
    top = jnp.maximum(a[0], b[0])
    ea = jnp.exp(a[0] - top)
    eb = jnp.exp(b[0] - top)
    return jnp.stack([top, a[1] * ea + b[1] * eb, a[2] * ea + b[2] * eb, a[3] + b[3]])


def xor_gather(x, axis, size, index):
    bit = 1
    while bit < size:
        other = lax.ppermute(x, axis, [(i, i ^ bit) for i in range(size)])
        upper = (index & bit) != 0
        x = jnp.concatenate([jnp.where(upper, other, x), jnp.where(upper, x, other)], axis=0)
        bit *= 2
    return x


def xor_reduce(x, axis, size, combine):
    bit = 1
    while bit < size:
        x = combine(x, lax.ppermute(x, axis, [(i, i ^ bit) for i in range(size)]))
        bit *= 2
    return x


def body(hidden, norm_gain, head_weight, token_ids, lengths, group_ids):
    req_dev, pos_dev, model_width = hidden.shape
    vocab_dev = head_weight.shape[1]
    n_chip = lax.axis_size("chip")
    n_core = lax.axis_size("core")
    n_req = lax.axis_size("req")
    chip = lax.axis_index("chip")
    core = lax.axis_index("core")
    req_index = lax.axis_index("req")
    values = hidden.astype(jnp.float32)
    squares = jnp.mean(values * values, axis=-1, keepdims=True)
    normed = (values * lax.rsqrt(squares + norm_eps) * norm_gain).astype(jnp.bfloat16)
    rows = lax.all_gather(normed, "chip", axis=1, tiled=True)
    other = lax.ppermute(head_weight, "core", [(0, 1), (1, 0)])
    first = core == 0
    weight = jnp.concatenate([jnp.where(first, head_weight, other), jnp.where(first, other, head_weight)], axis=1)
    offset = chip * (n_core * vocab_dev)
    half_len = rows.shape[1]
    tokens = xor_gather(token_ids.T, "chip", n_chip, chip)
    own_lengths = lax.dynamic_slice_in_dim(lengths, req_index * req_dev, req_dev)
    per_request = []
    for k in range(req_dev):
        blocks = []
        for start in range(0, half_len, BLOCK):
            size = min(BLOCK, half_len - start)
            blocks.append(block_stats(rows[k, start : start + size], tokens[start : start + size, k], weight, offset))
        per_request.append(jnp.concatenate(blocks, axis=1))
    stats = jnp.stack(per_request, axis=1)
    stats = xor_reduce(stats, "chip", n_chip, merge)
    row_top, exp_total, moment, token_logit = stats[0], stats[1], stats[2], stats[3]
    log_total = row_top + jnp.log(exp_total)
    raw_logprob = token_logit - log_total
    raw_entropy = log_total - moment / exp_total
    index = jnp.arange(half_len, dtype=jnp.int32)
    positions = ((index // pos_dev) * n_core + core) * pos_dev + index % pos_dev
    is_live = positions[None, :] < own_lengths[:, None]
    logprob = jnp.where(is_live, raw_logprob, 0.0)
    entropy = jnp.where(is_live, raw_entropy, 0.0)
    half_seq = jnp.sum(logprob, axis=1)
    own_seq = half_seq + lax.ppermute(half_seq, "core", [(0, 1), (1, 0)])
    request_count = lengths.shape[0]
    slots = jnp.arange(request_count, dtype=jnp.int32)
    global_rows = req_index * req_dev + jnp.arange(req_dev, dtype=jnp.int32)
    seq_sum = jnp.sum(jnp.where(slots[None, :] == global_rows[:, None], own_seq[:, None], 0.0), axis=0)
    seq_sum = xor_reduce(seq_sum, "req", n_req, jnp.add)
    same = (group_ids[:, None] == group_ids[None, :]).astype(jnp.float32)
    members = jnp.sum(same, axis=1)
    group_mean = jnp.sum(same * seq_sum[None, :], axis=1) / members
    spread = jnp.sum(same * (seq_sum[None, :] - group_mean[:, None]) ** 2, axis=1) / members
    group_std = jnp.maximum(jnp.sqrt(spread), 1.0)
    centered = (seq_sum - group_mean) / group_std
    own = chip * pos_dev
    return (
        lax.dynamic_slice_in_dim(logprob, own, pos_dev, axis=1),
        lax.dynamic_slice_in_dim(entropy, own, pos_dev, axis=1),
        centered,
    )


def solution(mesh):
    n_req, n_vocab = mesh.devices.shape
    split = Mesh(np.asarray(mesh.devices).reshape(n_req, n_vocab // 2, 2), ("req", "chip", "core"))
    vocab = ("chip", "core")
    return jax.shard_map(
        body,
        mesh=split,
        in_specs=(P("req", vocab, None), P(), P(None, vocab), P("req", vocab), P(), P()),
        out_specs=(P("req", vocab), P("req", vocab), P()),
        check_vma=False,
    )
```

```python
import jax
import jax.numpy as jnp
import numpy as np
from jax import lax
from jax.sharding import Mesh
from jax.sharding import PartitionSpec as P

norm_eps = 1e-06
BLOCK = 768


def block_stats(rows, tokens, weight, offset):
    logits = jnp.dot(rows, weight, preferred_element_type=jnp.float32)
    row_top = jnp.max(logits, axis=1)
    exps = jnp.exp(logits - row_top[:, None])
    exp_total = jnp.sum(exps, axis=1)
    moment = jnp.sum(exps * logits, axis=1)
    columns = jnp.arange(weight.shape[1], dtype=jnp.int32)
    picked = jnp.sum(jnp.where(columns[None, :] == (tokens - offset)[:, None], logits, 0.0), axis=1)
    return jnp.stack([row_top, exp_total, moment, picked])


def merge(a, b):
    top = jnp.maximum(a[0], b[0])
    ea = jnp.exp(a[0] - top)
    eb = jnp.exp(b[0] - top)
    return jnp.stack([top, a[1] * ea + b[1] * eb, a[2] * ea + b[2] * eb, a[3] + b[3]])


def xor_gather(x, axis, size, index):
    bit = 1
    while bit < size:
        other = lax.ppermute(x, axis, [(i, i ^ bit) for i in range(size)])
        upper = (index & bit) != 0
        x = jnp.concatenate([jnp.where(upper, other, x), jnp.where(upper, x, other)], axis=0)
        bit *= 2
    return x


def xor_reduce(x, axis, size, combine):
    bit = 1
    while bit < size:
        x = combine(x, lax.ppermute(x, axis, [(i, i ^ bit) for i in range(size)]))
        bit *= 2
    return x


def body(hidden, norm_gain, head_weight, token_ids, lengths, group_ids):
    req_dev, pos_dev, model_width = hidden.shape
    vocab_dev = head_weight.shape[1]
    n_chip = lax.axis_size("chip")
    n_core = lax.axis_size("core")
    n_req = lax.axis_size("req")
    chip = lax.axis_index("chip")
    core = lax.axis_index("core")
    req_index = lax.axis_index("req")
    values = hidden.astype(jnp.float32)
    squares = jnp.mean(values * values, axis=-1, keepdims=True)
    normed = (values * lax.rsqrt(squares + norm_eps) * norm_gain).astype(jnp.bfloat16)
    rows = lax.all_gather(normed, "chip", axis=1, tiled=True)
    other = lax.ppermute(head_weight, "core", [(0, 1), (1, 0)])
    first = core == 0
    weight = jnp.concatenate([jnp.where(first, head_weight, other), jnp.where(first, other, head_weight)], axis=1)
    weight = lax.optimization_barrier(weight)
    offset = chip * (n_core * vocab_dev)
    half_len = rows.shape[1]
    tokens = xor_gather(token_ids.T, "chip", n_chip, chip)
    own_lengths = lax.dynamic_slice_in_dim(lengths, req_index * req_dev, req_dev)
    per_request = []
    for k in range(req_dev):
        blocks = []
        for start in range(0, half_len, BLOCK):
            size = min(BLOCK, half_len - start)
            blocks.append(block_stats(rows[k, start : start + size], tokens[start : start + size, k], weight, offset))
        per_request.append(jnp.concatenate(blocks, axis=1))
    stats = jnp.stack(per_request, axis=1)
    stats = xor_reduce(stats, "chip", n_chip, merge)
    row_top, exp_total, moment, token_logit = stats[0], stats[1], stats[2], stats[3]
    log_total = row_top + jnp.log(exp_total)
    raw_logprob = token_logit - log_total
    raw_entropy = log_total - moment / exp_total
    index = jnp.arange(half_len, dtype=jnp.int32)
    positions = ((index // pos_dev) * n_core + core) * pos_dev + index % pos_dev
    is_live = positions[None, :] < own_lengths[:, None]
    logprob = jnp.where(is_live, raw_logprob, 0.0)
    entropy = jnp.where(is_live, raw_entropy, 0.0)
    half_seq = jnp.sum(logprob, axis=1)
    own_seq = half_seq + lax.ppermute(half_seq, "core", [(0, 1), (1, 0)])
    request_count = lengths.shape[0]
    slots = jnp.arange(request_count, dtype=jnp.int32)
    global_rows = req_index * req_dev + jnp.arange(req_dev, dtype=jnp.int32)
    seq_sum = jnp.sum(jnp.where(slots[None, :] == global_rows[:, None], own_seq[:, None], 0.0), axis=0)
    seq_sum = xor_reduce(seq_sum, "req", n_req, jnp.add)
    same = (group_ids[:, None] == group_ids[None, :]).astype(jnp.float32)
    members = jnp.sum(same, axis=1)
    group_mean = jnp.sum(same * seq_sum[None, :], axis=1) / members
    spread = jnp.sum(same * (seq_sum[None, :] - group_mean[:, None]) ** 2, axis=1) / members
    group_std = jnp.maximum(jnp.sqrt(spread), 1.0)
    centered = (seq_sum - group_mean) / group_std
    own = chip * pos_dev
    return (
        lax.dynamic_slice_in_dim(logprob, own, pos_dev, axis=1),
        lax.dynamic_slice_in_dim(entropy, own, pos_dev, axis=1),
        centered,
    )


def solution(mesh):
    n_req, n_vocab = mesh.devices.shape
    split = Mesh(np.asarray(mesh.devices).reshape(n_req, n_vocab // 2, 2), ("req", "chip", "core"))
    vocab = ("chip", "core")
    return jax.shard_map(
        body,
        mesh=split,
        in_specs=(P("req", vocab, None), P(), P(None, vocab), P("req", vocab), P(), P()),
        out_specs=(P("req", vocab), P("req", vocab), P()),
        check_vma=False,
    )
```

```python
import jax
import jax.numpy as jnp
import numpy as np
from jax import lax
from jax.sharding import Mesh
from jax.sharding import PartitionSpec as P

norm_eps = 1e-06
BLOCK = 1536


def block_stats(rows, tokens, weight, offset):
    logits = jnp.dot(rows, weight, preferred_element_type=jnp.float32)
    row_top = jnp.max(logits, axis=1)
    exps = jnp.exp(logits - row_top[:, None])
    exp_total = jnp.sum(exps, axis=1)
    moment = jnp.sum(exps * logits, axis=1)
    columns = jnp.arange(weight.shape[1], dtype=jnp.int32)
    picked = jnp.sum(jnp.where(columns[None, :] == (tokens - offset)[:, None], logits, 0.0), axis=1)
    return jnp.stack([row_top, exp_total, moment, picked])


def merge(a, b):
    top = jnp.maximum(a[0], b[0])
    ea = jnp.exp(a[0] - top)
    eb = jnp.exp(b[0] - top)
    return jnp.stack([top, a[1] * ea + b[1] * eb, a[2] * ea + b[2] * eb, a[3] + b[3]])


def xor_gather(x, axis, size, index):
    bit = 1
    while bit < size:
        other = lax.ppermute(x, axis, [(i, i ^ bit) for i in range(size)])
        upper = (index & bit) != 0
        x = jnp.concatenate([jnp.where(upper, other, x), jnp.where(upper, x, other)], axis=0)
        bit *= 2
    return x


def xor_reduce(x, axis, size, combine):
    bit = 1
    while bit < size:
        x = combine(x, lax.ppermute(x, axis, [(i, i ^ bit) for i in range(size)]))
        bit *= 2
    return x


def body(hidden, norm_gain, head_weight, token_ids, lengths, group_ids):
    req_dev, pos_dev, model_width = hidden.shape
    vocab_dev = head_weight.shape[1]
    n_chip = lax.axis_size("chip")
    n_core = lax.axis_size("core")
    n_req = lax.axis_size("req")
    chip = lax.axis_index("chip")
    core = lax.axis_index("core")
    req_index = lax.axis_index("req")
    values = hidden.astype(jnp.float32)
    squares = jnp.mean(values * values, axis=-1, keepdims=True)
    normed = (values * lax.rsqrt(squares + norm_eps) * norm_gain).astype(jnp.bfloat16)
    rows = lax.all_gather(normed, "chip", axis=1, tiled=True)
    other = lax.ppermute(head_weight, "core", [(0, 1), (1, 0)])
    first = core == 0
    weight = jnp.concatenate([jnp.where(first, head_weight, other), jnp.where(first, other, head_weight)], axis=1)
    weight = lax.optimization_barrier(weight)
    offset = chip * (n_core * vocab_dev)
    half_len = rows.shape[1]
    tokens = xor_gather(token_ids.T, "chip", n_chip, chip)
    own_lengths = lax.dynamic_slice_in_dim(lengths, req_index * req_dev, req_dev)
    flat_rows = rows.reshape(req_dev * half_len, model_width)
    flat_tokens = tokens.T.reshape(req_dev * half_len)
    blocks = []
    for start in range(0, req_dev * half_len, BLOCK):
        size = min(BLOCK, req_dev * half_len - start)
        blocks.append(block_stats(flat_rows[start : start + size], flat_tokens[start : start + size], weight, offset))
    stats = jnp.concatenate(blocks, axis=1).reshape(4, req_dev, half_len)
    stats = xor_reduce(stats, "chip", n_chip, merge)
    row_top, exp_total, moment, token_logit = stats[0], stats[1], stats[2], stats[3]
    log_total = row_top + jnp.log(exp_total)
    raw_logprob = token_logit - log_total
    raw_entropy = log_total - moment / exp_total
    index = jnp.arange(half_len, dtype=jnp.int32)
    positions = ((index // pos_dev) * n_core + core) * pos_dev + index % pos_dev
    is_live = positions[None, :] < own_lengths[:, None]
    logprob = jnp.where(is_live, raw_logprob, 0.0)
    entropy = jnp.where(is_live, raw_entropy, 0.0)
    half_seq = jnp.sum(logprob, axis=1)
    own_seq = half_seq + lax.ppermute(half_seq, "core", [(0, 1), (1, 0)])
    request_count = lengths.shape[0]
    slots = jnp.arange(request_count, dtype=jnp.int32)
    global_rows = req_index * req_dev + jnp.arange(req_dev, dtype=jnp.int32)
    seq_sum = jnp.sum(jnp.where(slots[None, :] == global_rows[:, None], own_seq[:, None], 0.0), axis=0)
    seq_sum = xor_reduce(seq_sum, "req", n_req, jnp.add)
    same = (group_ids[:, None] == group_ids[None, :]).astype(jnp.float32)
    members = jnp.sum(same, axis=1)
    group_mean = jnp.sum(same * seq_sum[None, :], axis=1) / members
    spread = jnp.sum(same * (seq_sum[None, :] - group_mean[:, None]) ** 2, axis=1) / members
    group_std = jnp.maximum(jnp.sqrt(spread), 1.0)
    centered = (seq_sum - group_mean) / group_std
    own = chip * pos_dev
    return (
        lax.dynamic_slice_in_dim(logprob, own, pos_dev, axis=1),
        lax.dynamic_slice_in_dim(entropy, own, pos_dev, axis=1),
        centered,
    )


def solution(mesh):
    n_req, n_vocab = mesh.devices.shape
    split = Mesh(np.asarray(mesh.devices).reshape(n_req, n_vocab // 2, 2), ("req", "chip", "core"))
    vocab = ("chip", "core")
    return jax.shard_map(
        body,
        mesh=split,
        in_specs=(P("req", vocab, None), P(), P(None, vocab), P("req", vocab), P(), P()),
        out_specs=(P("req", vocab), P("req", vocab), P()),
        check_vma=False,
    )
```

```python
import jax
import jax.numpy as jnp
import numpy as np
from jax import lax
from jax.sharding import Mesh
from jax.sharding import PartitionSpec as P

norm_eps = 1e-06
BLOCK = 1536


def block_stats(rows, tokens, weight, offset):
    logits = jnp.dot(rows, weight, preferred_element_type=jnp.float32)
    row_top = jnp.max(logits, axis=1)
    exps = jnp.exp(logits - row_top[:, None])
    exp_total = jnp.sum(exps, axis=1)
    moment = jnp.sum(exps * logits, axis=1)
    columns = jnp.arange(weight.shape[1], dtype=jnp.int32)
    picked = jnp.sum(jnp.where(columns[None, :] == (tokens - offset)[:, None], logits, 0.0), axis=1)
    return jnp.stack([row_top, exp_total, moment, picked])


def merge(a, b):
    top = jnp.maximum(a[0], b[0])
    ea = jnp.exp(a[0] - top)
    eb = jnp.exp(b[0] - top)
    return jnp.stack([top, a[1] * ea + b[1] * eb, a[2] * ea + b[2] * eb, a[3] + b[3]])


def xor_gather(x, axis, size, index):
    bit = 1
    while bit < size:
        other = lax.ppermute(x, axis, [(i, i ^ bit) for i in range(size)])
        upper = (index & bit) != 0
        x = jnp.concatenate([jnp.where(upper, other, x), jnp.where(upper, x, other)], axis=0)
        bit *= 2
    return x


def xor_reduce(x, axis, size, combine):
    bit = 1
    while bit < size:
        x = combine(x, lax.ppermute(x, axis, [(i, i ^ bit) for i in range(size)]))
        bit *= 2
    return x


def body(hidden, norm_gain, head_weight, token_ids, lengths, group_ids):
    req_dev, pos_dev, model_width = hidden.shape
    vocab_dev = head_weight.shape[1]
    n_chip = lax.axis_size("chip")
    n_core = lax.axis_size("core")
    n_req = lax.axis_size("req")
    chip = lax.axis_index("chip")
    core = lax.axis_index("core")
    req_index = lax.axis_index("req")
    values = hidden.astype(jnp.float32)
    squares = jnp.mean(values * values, axis=-1, keepdims=True)
    normed = (values * lax.rsqrt(squares + norm_eps) * norm_gain).astype(jnp.bfloat16)
    own_rows = req_dev * pos_dev
    flat_rows = lax.all_gather(normed.reshape(own_rows, model_width), "chip", axis=0, tiled=True)
    other = lax.ppermute(head_weight, "core", [(0, 1), (1, 0)])
    first = core == 0
    weight = jnp.concatenate([jnp.where(first, head_weight, other), jnp.where(first, other, head_weight)], axis=1)
    weight = lax.optimization_barrier(weight)
    offset = chip * (n_core * vocab_dev)
    half_len = n_chip * pos_dev
    flat_tokens = xor_gather(token_ids, "chip", n_chip, chip).reshape(n_chip * own_rows)
    own_lengths = lax.dynamic_slice_in_dim(lengths, req_index * req_dev, req_dev)
    blocks = []
    for start in range(0, req_dev * half_len, BLOCK):
        size = min(BLOCK, req_dev * half_len - start)
        blocks.append(block_stats(flat_rows[start : start + size], flat_tokens[start : start + size], weight, offset))
    stats = jnp.concatenate(blocks, axis=1).reshape(4, n_chip, req_dev, pos_dev)
    stats = stats.transpose(0, 2, 1, 3).reshape(4, req_dev, half_len)
    stats = xor_reduce(stats, "chip", n_chip, merge)
    row_top, exp_total, moment, token_logit = stats[0], stats[1], stats[2], stats[3]
    log_total = row_top + jnp.log(exp_total)
    raw_logprob = token_logit - log_total
    raw_entropy = log_total - moment / exp_total
    index = jnp.arange(half_len, dtype=jnp.int32)
    positions = ((index // pos_dev) * n_core + core) * pos_dev + index % pos_dev
    is_live = positions[None, :] < own_lengths[:, None]
    logprob = jnp.where(is_live, raw_logprob, 0.0)
    entropy = jnp.where(is_live, raw_entropy, 0.0)
    half_seq = jnp.sum(logprob, axis=1)
    own_seq = half_seq + lax.ppermute(half_seq, "core", [(0, 1), (1, 0)])
    request_count = lengths.shape[0]
    slots = jnp.arange(request_count, dtype=jnp.int32)
    global_rows = req_index * req_dev + jnp.arange(req_dev, dtype=jnp.int32)
    seq_sum = jnp.sum(jnp.where(slots[None, :] == global_rows[:, None], own_seq[:, None], 0.0), axis=0)
    seq_sum = xor_reduce(seq_sum, "req", n_req, jnp.add)
    same = (group_ids[:, None] == group_ids[None, :]).astype(jnp.float32)
    members = jnp.sum(same, axis=1)
    group_mean = jnp.sum(same * seq_sum[None, :], axis=1) / members
    spread = jnp.sum(same * (seq_sum[None, :] - group_mean[:, None]) ** 2, axis=1) / members
    group_std = jnp.maximum(jnp.sqrt(spread), 1.0)
    centered = (seq_sum - group_mean) / group_std
    own = chip * pos_dev
    return (
        lax.dynamic_slice_in_dim(logprob, own, pos_dev, axis=1),
        lax.dynamic_slice_in_dim(entropy, own, pos_dev, axis=1),
        centered,
    )


def solution(mesh):
    n_req, n_vocab = mesh.devices.shape
    split = Mesh(np.asarray(mesh.devices).reshape(n_req, n_vocab // 2, 2), ("req", "chip", "core"))
    vocab = ("chip", "core")
    return jax.shard_map(
        body,
        mesh=split,
        in_specs=(P("req", vocab, None), P(), P(None, vocab), P("req", vocab), P(), P()),
        out_specs=(P("req", vocab), P("req", vocab), P()),
        check_vma=False,
    )
```

```python
import jax
import jax.numpy as jnp
import numpy as np
from jax import lax
from jax.sharding import Mesh
from jax.sharding import PartitionSpec as P

norm_eps = 1e-06
BLOCK = 1536


def block_stats(rows, tokens, weight, offset):
    logits = jnp.dot(rows, weight, preferred_element_type=jnp.float32)
    row_top = jnp.max(logits, axis=1)
    exps = jnp.exp(logits - row_top[:, None])
    exp_total = jnp.sum(exps, axis=1)
    moment = jnp.sum(exps * logits, axis=1)
    columns = jnp.arange(weight.shape[1], dtype=jnp.int32)
    picked = jnp.sum(jnp.where(columns[None, :] == (tokens - offset)[:, None], logits, 0.0), axis=1)
    return jnp.stack([row_top, exp_total, moment, picked])


def merge(a, b):
    top = jnp.maximum(a[0], b[0])
    ea = jnp.exp(a[0] - top)
    eb = jnp.exp(b[0] - top)
    return jnp.stack([top, a[1] * ea + b[1] * eb, a[2] * ea + b[2] * eb, a[3] + b[3]])


def xor_gather(x, axis, size, index):
    bit = 1
    while bit < size:
        other = lax.ppermute(x, axis, [(i, i ^ bit) for i in range(size)])
        upper = (index & bit) != 0
        x = jnp.concatenate([jnp.where(upper, other, x), jnp.where(upper, x, other)], axis=0)
        bit *= 2
    return x


def xor_reduce(x, axis, size, combine):
    bit = 1
    while bit < size:
        x = combine(x, lax.ppermute(x, axis, [(i, i ^ bit) for i in range(size)]))
        bit *= 2
    return x


def shift_gather(v, axis, n, index):
    got = [v] + [lax.ppermute(v, axis, [(i, (i + d) % n) for i in range(n)]) for d in range(1, n)]
    order = (index - jnp.arange(n, dtype=jnp.int32)) % n
    return jnp.take(jnp.stack(got), order, axis=0)


def body(hidden, norm_gain, head_weight, token_ids, lengths, group_ids):
    req_dev, pos_dev, model_width = hidden.shape
    vocab_dev = head_weight.shape[1]
    chips = ("y", "x")
    n_chip = lax.axis_size(chips)
    n_core = lax.axis_size("core")
    n_req = lax.axis_size("req")
    chip = lax.axis_index(chips)
    core = lax.axis_index("core")
    req_index = lax.axis_index("req")
    values = hidden.astype(jnp.float32)
    squares = jnp.mean(values * values, axis=-1, keepdims=True)
    normed = (values * lax.rsqrt(squares + norm_eps) * norm_gain).astype(jnp.bfloat16)
    n_y, n_x = lax.axis_size("y"), lax.axis_size("x")
    y_index, x_index = lax.axis_index("y"), lax.axis_index("x")
    half_req = req_dev // 2
    half_rows = half_req * pos_dev
    rows_a = lax.all_gather(normed[:half_req].reshape(half_rows, model_width), chips, axis=0, tiled=True)
    part_b = shift_gather(normed[half_req:].reshape(half_rows, model_width), "y", n_y, y_index)
    rows_b = shift_gather(part_b, "x", n_x, x_index).reshape(n_chip * half_rows, model_width)
    other = lax.ppermute(head_weight, "core", [(0, 1), (1, 0)])
    first = core == 0
    weight = jnp.concatenate([jnp.where(first, head_weight, other), jnp.where(first, other, head_weight)], axis=1)
    weight = lax.optimization_barrier(weight)
    offset = chip * (n_core * vocab_dev)
    half_len = n_chip * pos_dev
    tok = xor_gather(token_ids, chips, n_chip, chip).reshape(n_y, n_x, req_dev, pos_dev)
    tok_a = tok[:, :, :half_req].reshape(-1)
    tok_b = tok[:, :, half_req:].transpose(1, 0, 2, 3).reshape(-1)
    own_lengths = lax.dynamic_slice_in_dim(lengths, req_index * req_dev, req_dev)
    stats_b = block_stats(rows_b, tok_b, weight, offset).reshape(4, n_x, n_y, half_req, pos_dev)
    stats_b = stats_b.transpose(0, 2, 1, 3, 4).reshape(4, n_chip, half_req, pos_dev)
    stats_a = block_stats(rows_a, tok_a, weight, offset).reshape(4, n_chip, half_req, pos_dev)
    stats = jnp.concatenate([stats_a, stats_b], axis=2)
    stats = stats.transpose(0, 2, 1, 3).reshape(4, req_dev, half_len)
    stats = xor_reduce(stats, chips, n_chip, merge)
    row_top, exp_total, moment, token_logit = stats[0], stats[1], stats[2], stats[3]
    log_total = row_top + jnp.log(exp_total)
    raw_logprob = token_logit - log_total
    raw_entropy = log_total - moment / exp_total
    index = jnp.arange(half_len, dtype=jnp.int32)
    positions = ((index // pos_dev) * n_core + core) * pos_dev + index % pos_dev
    is_live = positions[None, :] < own_lengths[:, None]
    logprob = jnp.where(is_live, raw_logprob, 0.0)
    entropy = jnp.where(is_live, raw_entropy, 0.0)
    half_seq = jnp.sum(logprob, axis=1)
    own_seq = half_seq + lax.ppermute(half_seq, "core", [(0, 1), (1, 0)])
    request_count = lengths.shape[0]
    slots = jnp.arange(request_count, dtype=jnp.int32)
    global_rows = req_index * req_dev + jnp.arange(req_dev, dtype=jnp.int32)
    seq_sum = jnp.sum(jnp.where(slots[None, :] == global_rows[:, None], own_seq[:, None], 0.0), axis=0)
    seq_sum = xor_reduce(seq_sum, "req", n_req, jnp.add)
    same = (group_ids[:, None] == group_ids[None, :]).astype(jnp.float32)
    members = jnp.sum(same, axis=1)
    group_mean = jnp.sum(same * seq_sum[None, :], axis=1) / members
    spread = jnp.sum(same * (seq_sum[None, :] - group_mean[:, None]) ** 2, axis=1) / members
    group_std = jnp.maximum(jnp.sqrt(spread), 1.0)
    centered = (seq_sum - group_mean) / group_std
    own = chip * pos_dev
    return (
        lax.dynamic_slice_in_dim(logprob, own, pos_dev, axis=1),
        lax.dynamic_slice_in_dim(entropy, own, pos_dev, axis=1),
        centered,
    )


def solution(mesh):
    n_req, n_vocab = mesh.devices.shape
    side = int(round((n_vocab // 2) ** 0.5))
    split = Mesh(np.asarray(mesh.devices).reshape(n_req, side, n_vocab // 2 // side, 2), ("req", "y", "x", "core"))
    vocab = ("y", "x", "core")
    return jax.shard_map(
        body,
        mesh=split,
        in_specs=(P("req", vocab, None), P(), P(None, vocab), P("req", vocab), P(), P()),
        out_specs=(P("req", vocab), P("req", vocab), P()),
        check_vma=False,
    )
```

```python
import functools

import jax
import jax.numpy as jnp
import numpy as np
from jax import lax
from jax.experimental import pallas as pl
from jax.experimental.pallas import tpu as pltpu
from jax.sharding import Mesh
from jax.sharding import PartitionSpec as P

norm_eps = 1e-06
TILE = 256


def stats_kernel(real_cols, rows_ref, w_ref, ids_ref, out_ref):
    raw = jnp.dot(rows_ref[...], w_ref[...], preferred_element_type=jnp.float32)
    cols = lax.broadcasted_iota(jnp.int32, raw.shape, 1)
    masked = jnp.where(cols < real_cols, raw, -jnp.inf)
    top = jnp.max(masked, axis=1, keepdims=True)
    exps = jnp.exp(masked - top)
    out_ref[:, 0:1] = top
    out_ref[:, 1:2] = jnp.sum(exps, axis=1, keepdims=True)
    out_ref[:, 2:3] = jnp.sum(exps * raw, axis=1, keepdims=True)
    out_ref[:, 3:4] = jnp.sum(jnp.where(cols == ids_ref[...], raw, 0.0), axis=1, keepdims=True)


def kernel_stats(rows, weight, local_ids, real_cols):
    n, d = rows.shape
    c = weight.shape[1]
    return pl.pallas_call(
        functools.partial(stats_kernel, real_cols),
        grid=(n // TILE,),
        in_specs=[
            pl.BlockSpec((TILE, d), lambda i: (i, 0)),
            pl.BlockSpec((d, c), lambda i: (0, 0)),
            pl.BlockSpec((TILE, 1), lambda i: (i, 0)),
        ],
        out_specs=pl.BlockSpec((TILE, 4), lambda i: (i, 0)),
        out_shape=jax.ShapeDtypeStruct((n, 4), jnp.float32),
        compiler_params=pltpu.CompilerParams(vmem_limit_bytes=48 * 1024 * 1024),
        cost_estimate=pl.CostEstimate(flops=2 * n * d * c, transcendentals=n * c, bytes_accessed=2 * (n * d + d * c) + 20 * n),
    )(rows, weight, local_ids)


def merge(a, b):
    top = jnp.maximum(a[0], b[0])
    ea = jnp.exp(a[0] - top)
    eb = jnp.exp(b[0] - top)
    return jnp.stack([top, a[1] * ea + b[1] * eb, a[2] * ea + b[2] * eb, a[3] + b[3]])


def xor_gather(x, axis, size, index):
    bit = 1
    while bit < size:
        other = lax.ppermute(x, axis, [(i, i ^ bit) for i in range(size)])
        upper = (index & bit) != 0
        x = jnp.concatenate([jnp.where(upper, other, x), jnp.where(upper, x, other)], axis=0)
        bit *= 2
    return x


def xor_reduce(x, axis, size, combine):
    bit = 1
    while bit < size:
        x = combine(x, lax.ppermute(x, axis, [(i, i ^ bit) for i in range(size)]))
        bit *= 2
    return x


def body(hidden, norm_gain, head_weight, token_ids, lengths, group_ids):
    req_dev, pos_dev, model_width = hidden.shape
    vocab_dev = head_weight.shape[1]
    n_chip = lax.axis_size("chip")
    n_core = lax.axis_size("core")
    n_req = lax.axis_size("req")
    chip = lax.axis_index("chip")
    core = lax.axis_index("core")
    req_index = lax.axis_index("req")
    values = hidden.astype(jnp.float32)
    squares = jnp.mean(values * values, axis=-1, keepdims=True)
    normed = (values * lax.rsqrt(squares + norm_eps) * norm_gain).astype(jnp.bfloat16)
    own_rows = req_dev * pos_dev
    flat_rows = lax.all_gather(normed.reshape(own_rows, model_width), "chip", axis=0, tiled=True)
    other = lax.ppermute(head_weight, "core", [(0, 1), (1, 0)])
    first = core == 0
    weight = jnp.concatenate([jnp.where(first, head_weight, other), jnp.where(first, other, head_weight)], axis=1)
    cols = weight.shape[1]
    weight = jnp.pad(weight, ((0, 0), (0, -cols % 128)))
    weight = lax.optimization_barrier(weight)
    offset = chip * (n_core * vocab_dev)
    half_len = n_chip * pos_dev
    flat_tokens = xor_gather(token_ids, "chip", n_chip, chip).reshape(n_chip * own_rows)
    own_lengths = lax.dynamic_slice_in_dim(lengths, req_index * req_dev, req_dev)
    local_ids = (flat_tokens - offset).reshape(-1, 1)
    stats = kernel_stats(flat_rows, weight, local_ids, cols).T.reshape(4, n_chip, req_dev, pos_dev)
    stats = stats.transpose(0, 2, 1, 3).reshape(4, req_dev, half_len)
    stats = xor_reduce(stats, "chip", n_chip, merge)
    row_top, exp_total, moment, token_logit = stats[0], stats[1], stats[2], stats[3]
    log_total = row_top + jnp.log(exp_total)
    raw_logprob = token_logit - log_total
    raw_entropy = log_total - moment / exp_total
    index = jnp.arange(half_len, dtype=jnp.int32)
    positions = ((index // pos_dev) * n_core + core) * pos_dev + index % pos_dev
    is_live = positions[None, :] < own_lengths[:, None]
    logprob = jnp.where(is_live, raw_logprob, 0.0)
    entropy = jnp.where(is_live, raw_entropy, 0.0)
    half_seq = jnp.sum(logprob, axis=1)
    own_seq = half_seq + lax.ppermute(half_seq, "core", [(0, 1), (1, 0)])
    request_count = lengths.shape[0]
    slots = jnp.arange(request_count, dtype=jnp.int32)
    global_rows = req_index * req_dev + jnp.arange(req_dev, dtype=jnp.int32)
    seq_sum = jnp.sum(jnp.where(slots[None, :] == global_rows[:, None], own_seq[:, None], 0.0), axis=0)
    seq_sum = xor_reduce(seq_sum, "req", n_req, jnp.add)
    same = (group_ids[:, None] == group_ids[None, :]).astype(jnp.float32)
    members = jnp.sum(same, axis=1)
    group_mean = jnp.sum(same * seq_sum[None, :], axis=1) / members
    spread = jnp.sum(same * (seq_sum[None, :] - group_mean[:, None]) ** 2, axis=1) / members
    group_std = jnp.maximum(jnp.sqrt(spread), 1.0)
    centered = (seq_sum - group_mean) / group_std
    own = chip * pos_dev
    return (
        lax.dynamic_slice_in_dim(logprob, own, pos_dev, axis=1),
        lax.dynamic_slice_in_dim(entropy, own, pos_dev, axis=1),
        centered,
    )


def solution(mesh):
    n_req, n_vocab = mesh.devices.shape
    split = Mesh(np.asarray(mesh.devices).reshape(n_req, n_vocab // 2, 2), ("req", "chip", "core"))
    vocab = ("chip", "core")
    return jax.shard_map(
        body,
        mesh=split,
        in_specs=(P("req", vocab, None), P(), P(None, vocab), P("req", vocab), P(), P()),
        out_specs=(P("req", vocab), P("req", vocab), P()),
        check_vma=False,
    )
```

```python
import functools

import jax
import jax.numpy as jnp
import numpy as np
from jax import lax
from jax.experimental import pallas as pl
from jax.experimental.pallas import tpu as pltpu
from jax.sharding import Mesh
from jax.sharding import PartitionSpec as P

norm_eps = 1e-06
TILE = 256


def stats_kernel(real_cols, rows_ref, w_ref, ids_ref, out_ref):
    raw = lax.dot_general(w_ref[...], rows_ref[...], (((0,), (1,)), ((), ())), preferred_element_type=jnp.float32)
    cols = lax.broadcasted_iota(jnp.int32, raw.shape, 0)
    masked = jnp.where(cols < real_cols, raw, -jnp.inf)
    top = jnp.max(masked, axis=0, keepdims=True)
    exps = jnp.exp(masked - top)
    out_ref[0:1, :] = top
    out_ref[1:2, :] = jnp.sum(exps, axis=0, keepdims=True)
    out_ref[2:3, :] = jnp.sum(exps * raw, axis=0, keepdims=True)
    out_ref[3:4, :] = jnp.sum(jnp.where(cols == ids_ref[...], raw, 0.0), axis=0, keepdims=True)


def kernel_stats(rows, weight, local_ids, real_cols):
    n, d = rows.shape
    c = weight.shape[1]
    return pl.pallas_call(
        functools.partial(stats_kernel, real_cols),
        grid=(n // TILE,),
        in_specs=[
            pl.BlockSpec((TILE, d), lambda i: (i, 0)),
            pl.BlockSpec((d, c), lambda i: (0, 0)),
            pl.BlockSpec((1, TILE), lambda i: (0, i)),
        ],
        out_specs=pl.BlockSpec((4, TILE), lambda i: (0, i)),
        out_shape=jax.ShapeDtypeStruct((4, n), jnp.float32),
        compiler_params=pltpu.CompilerParams(vmem_limit_bytes=48 * 1024 * 1024),
        cost_estimate=pl.CostEstimate(flops=2 * n * d * c, transcendentals=n * c, bytes_accessed=2 * (n * d + d * c) + 20 * n),
    )(rows, weight, local_ids)


def merge(a, b):
    top = jnp.maximum(a[0], b[0])
    ea = jnp.exp(a[0] - top)
    eb = jnp.exp(b[0] - top)
    return jnp.stack([top, a[1] * ea + b[1] * eb, a[2] * ea + b[2] * eb, a[3] + b[3]])


def xor_gather(x, axis, size, index):
    bit = 1
    while bit < size:
        other = lax.ppermute(x, axis, [(i, i ^ bit) for i in range(size)])
        upper = (index & bit) != 0
        x = jnp.concatenate([jnp.where(upper, other, x), jnp.where(upper, x, other)], axis=0)
        bit *= 2
    return x


def xor_reduce(x, axis, size, combine):
    bit = 1
    while bit < size:
        x = combine(x, lax.ppermute(x, axis, [(i, i ^ bit) for i in range(size)]))
        bit *= 2
    return x


def body(hidden, norm_gain, head_weight, token_ids, lengths, group_ids):
    req_dev, pos_dev, model_width = hidden.shape
    vocab_dev = head_weight.shape[1]
    n_chip = lax.axis_size("chip")
    n_core = lax.axis_size("core")
    n_req = lax.axis_size("req")
    chip = lax.axis_index("chip")
    core = lax.axis_index("core")
    req_index = lax.axis_index("req")
    values = hidden.astype(jnp.float32)
    squares = jnp.mean(values * values, axis=-1, keepdims=True)
    normed = (values * lax.rsqrt(squares + norm_eps) * norm_gain).astype(jnp.bfloat16)
    own_rows = req_dev * pos_dev
    flat_rows = lax.all_gather(normed.reshape(own_rows, model_width), "chip", axis=0, tiled=True)
    other = lax.ppermute(head_weight, "core", [(0, 1), (1, 0)])
    first = core == 0
    weight = jnp.concatenate([jnp.where(first, head_weight, other), jnp.where(first, other, head_weight)], axis=1)
    cols = weight.shape[1]
    weight = jnp.pad(weight, ((0, 0), (0, -cols % 128)))
    weight = lax.optimization_barrier(weight)
    offset = chip * (n_core * vocab_dev)
    half_len = n_chip * pos_dev
    flat_tokens = xor_gather(token_ids, "chip", n_chip, chip).reshape(n_chip * own_rows)
    own_lengths = lax.dynamic_slice_in_dim(lengths, req_index * req_dev, req_dev)
    local_ids = (flat_tokens - offset).reshape(1, -1)
    stats = kernel_stats(flat_rows, weight, local_ids, cols).reshape(4, n_chip, req_dev, pos_dev)
    stats = stats.transpose(0, 2, 1, 3).reshape(4, req_dev, half_len)
    stats = xor_reduce(stats, "chip", n_chip, merge)
    row_top, exp_total, moment, token_logit = stats[0], stats[1], stats[2], stats[3]
    log_total = row_top + jnp.log(exp_total)
    raw_logprob = token_logit - log_total
    raw_entropy = log_total - moment / exp_total
    index = jnp.arange(half_len, dtype=jnp.int32)
    positions = ((index // pos_dev) * n_core + core) * pos_dev + index % pos_dev
    is_live = positions[None, :] < own_lengths[:, None]
    logprob = jnp.where(is_live, raw_logprob, 0.0)
    entropy = jnp.where(is_live, raw_entropy, 0.0)
    half_seq = jnp.sum(logprob, axis=1)
    own_seq = half_seq + lax.ppermute(half_seq, "core", [(0, 1), (1, 0)])
    request_count = lengths.shape[0]
    slots = jnp.arange(request_count, dtype=jnp.int32)
    global_rows = req_index * req_dev + jnp.arange(req_dev, dtype=jnp.int32)
    seq_sum = jnp.sum(jnp.where(slots[None, :] == global_rows[:, None], own_seq[:, None], 0.0), axis=0)
    seq_sum = xor_reduce(seq_sum, "req", n_req, jnp.add)
    same = (group_ids[:, None] == group_ids[None, :]).astype(jnp.float32)
    members = jnp.sum(same, axis=1)
    group_mean = jnp.sum(same * seq_sum[None, :], axis=1) / members
    spread = jnp.sum(same * (seq_sum[None, :] - group_mean[:, None]) ** 2, axis=1) / members
    group_std = jnp.maximum(jnp.sqrt(spread), 1.0)
    centered = (seq_sum - group_mean) / group_std
    own = chip * pos_dev
    return (
        lax.dynamic_slice_in_dim(logprob, own, pos_dev, axis=1),
        lax.dynamic_slice_in_dim(entropy, own, pos_dev, axis=1),
        centered,
    )


def solution(mesh):
    n_req, n_vocab = mesh.devices.shape
    split = Mesh(np.asarray(mesh.devices).reshape(n_req, n_vocab // 2, 2), ("req", "chip", "core"))
    vocab = ("chip", "core")
    return jax.shard_map(
        body,
        mesh=split,
        in_specs=(P("req", vocab, None), P(), P(None, vocab), P("req", vocab), P(), P()),
        out_specs=(P("req", vocab), P("req", vocab), P()),
        check_vma=False,
    )
```

```python
import functools

import jax
import jax.numpy as jnp
import numpy as np
from jax import lax
from jax.experimental import pallas as pl
from jax.experimental.pallas import tpu as pltpu
from jax.sharding import Mesh
from jax.sharding import PartitionSpec as P

norm_eps = 1e-06
TILE = 512


def stats_kernel(real_cols, rows_ref, w_ref, ids_ref, out_ref):
    raw = lax.dot_general(w_ref[...], rows_ref[...], (((0,), (1,)), ((), ())), preferred_element_type=jnp.float32)
    cols = lax.broadcasted_iota(jnp.int32, raw.shape, 0)
    masked = jnp.where(cols < real_cols, raw, -jnp.inf)
    top = jnp.max(masked, axis=0, keepdims=True)
    exps = jnp.exp(masked - top)
    out_ref[0:1, :] = top
    out_ref[1:2, :] = jnp.sum(exps, axis=0, keepdims=True)
    out_ref[2:3, :] = jnp.sum(exps * raw, axis=0, keepdims=True)
    out_ref[3:4, :] = jnp.sum(jnp.where(cols == ids_ref[...], raw, 0.0), axis=0, keepdims=True)


def kernel_stats(rows, weight, local_ids, real_cols):
    n, d = rows.shape
    c = weight.shape[1]
    return pl.pallas_call(
        functools.partial(stats_kernel, real_cols),
        grid=(n // TILE,),
        in_specs=[
            pl.BlockSpec((TILE, d), lambda i: (i, 0)),
            pl.BlockSpec((d, c), lambda i: (0, 0)),
            pl.BlockSpec((1, TILE), lambda i: (0, i)),
        ],
        out_specs=pl.BlockSpec((4, TILE), lambda i: (0, i)),
        out_shape=jax.ShapeDtypeStruct((4, n), jnp.float32),
        compiler_params=pltpu.CompilerParams(vmem_limit_bytes=48 * 1024 * 1024),
        cost_estimate=pl.CostEstimate(flops=2 * n * d * c, transcendentals=n * c, bytes_accessed=2 * (n * d + d * c) + 20 * n),
    )(rows, weight, local_ids)


def merge(a, b):
    top = jnp.maximum(a[0], b[0])
    ea = jnp.exp(a[0] - top)
    eb = jnp.exp(b[0] - top)
    return jnp.stack([top, a[1] * ea + b[1] * eb, a[2] * ea + b[2] * eb, a[3] + b[3]])


def xor_gather(x, axis, size, index):
    bit = 1
    while bit < size:
        other = lax.ppermute(x, axis, [(i, i ^ bit) for i in range(size)])
        upper = (index & bit) != 0
        x = jnp.concatenate([jnp.where(upper, other, x), jnp.where(upper, x, other)], axis=0)
        bit *= 2
    return x


def xor_reduce(x, axis, size, combine):
    bit = 1
    while bit < size:
        x = combine(x, lax.ppermute(x, axis, [(i, i ^ bit) for i in range(size)]))
        bit *= 2
    return x


def body(hidden, norm_gain, head_weight, token_ids, lengths, group_ids):
    req_dev, pos_dev, model_width = hidden.shape
    vocab_dev = head_weight.shape[1]
    n_chip = lax.axis_size("chip")
    n_core = lax.axis_size("core")
    n_req = lax.axis_size("req")
    chip = lax.axis_index("chip")
    core = lax.axis_index("core")
    req_index = lax.axis_index("req")
    values = hidden.astype(jnp.float32)
    squares = jnp.mean(values * values, axis=-1, keepdims=True)
    normed = (values * lax.rsqrt(squares + norm_eps) * norm_gain).astype(jnp.bfloat16)
    own_rows = req_dev * pos_dev
    flat_rows = lax.all_gather(normed.reshape(own_rows, model_width), "chip", axis=0, tiled=True)
    other = lax.ppermute(head_weight, "core", [(0, 1), (1, 0)])
    first = core == 0
    weight = jnp.concatenate([jnp.where(first, head_weight, other), jnp.where(first, other, head_weight)], axis=1)
    cols = weight.shape[1]
    weight = jnp.pad(weight, ((0, 0), (0, -cols % 128)))
    weight = lax.optimization_barrier(weight)
    offset = chip * (n_core * vocab_dev)
    half_len = n_chip * pos_dev
    flat_tokens = xor_gather(token_ids, "chip", n_chip, chip).reshape(n_chip * own_rows)
    own_lengths = lax.dynamic_slice_in_dim(lengths, req_index * req_dev, req_dev)
    local_ids = (flat_tokens - offset).reshape(1, -1)
    stats = kernel_stats(flat_rows, weight, local_ids, cols).reshape(4, n_chip, req_dev, pos_dev)
    stats = stats.transpose(0, 2, 1, 3).reshape(4, req_dev, half_len)
    stats = xor_reduce(stats, "chip", n_chip, merge)
    row_top, exp_total, moment, token_logit = stats[0], stats[1], stats[2], stats[3]
    log_total = row_top + jnp.log(exp_total)
    raw_logprob = token_logit - log_total
    raw_entropy = log_total - moment / exp_total
    index = jnp.arange(half_len, dtype=jnp.int32)
    positions = ((index // pos_dev) * n_core + core) * pos_dev + index % pos_dev
    is_live = positions[None, :] < own_lengths[:, None]
    logprob = jnp.where(is_live, raw_logprob, 0.0)
    entropy = jnp.where(is_live, raw_entropy, 0.0)
    half_seq = jnp.sum(logprob, axis=1)
    own_seq = half_seq + lax.ppermute(half_seq, "core", [(0, 1), (1, 0)])
    request_count = lengths.shape[0]
    slots = jnp.arange(request_count, dtype=jnp.int32)
    global_rows = req_index * req_dev + jnp.arange(req_dev, dtype=jnp.int32)
    seq_sum = jnp.sum(jnp.where(slots[None, :] == global_rows[:, None], own_seq[:, None], 0.0), axis=0)
    seq_sum = xor_reduce(seq_sum, "req", n_req, jnp.add)
    same = (group_ids[:, None] == group_ids[None, :]).astype(jnp.float32)
    members = jnp.sum(same, axis=1)
    group_mean = jnp.sum(same * seq_sum[None, :], axis=1) / members
    spread = jnp.sum(same * (seq_sum[None, :] - group_mean[:, None]) ** 2, axis=1) / members
    group_std = jnp.maximum(jnp.sqrt(spread), 1.0)
    centered = (seq_sum - group_mean) / group_std
    own = chip * pos_dev
    return (
        lax.dynamic_slice_in_dim(logprob, own, pos_dev, axis=1),
        lax.dynamic_slice_in_dim(entropy, own, pos_dev, axis=1),
        centered,
    )


def solution(mesh):
    n_req, n_vocab = mesh.devices.shape
    split = Mesh(np.asarray(mesh.devices).reshape(n_req, n_vocab // 2, 2), ("req", "chip", "core"))
    vocab = ("chip", "core")
    return jax.shard_map(
        body,
        mesh=split,
        in_specs=(P("req", vocab, None), P(), P(None, vocab), P("req", vocab), P(), P()),
        out_specs=(P("req", vocab), P("req", vocab), P()),
        check_vma=False,
    )
```

```python
import functools

import jax
import jax.numpy as jnp
import numpy as np
from jax import lax
from jax.experimental import pallas as pl
from jax.experimental.pallas import tpu as pltpu
from jax.sharding import Mesh
from jax.sharding import PartitionSpec as P

norm_eps = 1e-06
TILE = 1024


def stats_kernel(real_cols, rows_ref, w_ref, ids_ref, out_ref):
    raw = lax.dot_general(w_ref[...], rows_ref[...], (((0,), (1,)), ((), ())), preferred_element_type=jnp.float32)
    cols = lax.broadcasted_iota(jnp.int32, raw.shape, 0)
    masked = jnp.where(cols < real_cols, raw, -jnp.inf)
    top = jnp.max(masked, axis=0, keepdims=True)
    exps = jnp.exp(masked - top)
    out_ref[0:1, :] = top
    out_ref[1:2, :] = jnp.sum(exps, axis=0, keepdims=True)
    out_ref[2:3, :] = jnp.sum(exps * raw, axis=0, keepdims=True)
    out_ref[3:4, :] = jnp.sum(jnp.where(cols == ids_ref[...], raw, 0.0), axis=0, keepdims=True)


def kernel_stats(rows, weight, local_ids, real_cols):
    n, d = rows.shape
    c = weight.shape[1]
    return pl.pallas_call(
        functools.partial(stats_kernel, real_cols),
        grid=(n // TILE,),
        in_specs=[
            pl.BlockSpec((TILE, d), lambda i: (i, 0)),
            pl.BlockSpec((d, c), lambda i: (0, 0)),
            pl.BlockSpec((1, TILE), lambda i: (0, i)),
        ],
        out_specs=pl.BlockSpec((4, TILE), lambda i: (0, i)),
        out_shape=jax.ShapeDtypeStruct((4, n), jnp.float32),
        compiler_params=pltpu.CompilerParams(vmem_limit_bytes=60 * 1024 * 1024),
        cost_estimate=pl.CostEstimate(flops=2 * n * d * c, transcendentals=n * c, bytes_accessed=2 * (n * d + d * c) + 20 * n),
    )(rows, weight, local_ids)


def merge(a, b):
    top = jnp.maximum(a[0], b[0])
    ea = jnp.exp(a[0] - top)
    eb = jnp.exp(b[0] - top)
    return jnp.stack([top, a[1] * ea + b[1] * eb, a[2] * ea + b[2] * eb, a[3] + b[3]])


def xor_gather(x, axis, size, index):
    bit = 1
    while bit < size:
        other = lax.ppermute(x, axis, [(i, i ^ bit) for i in range(size)])
        upper = (index & bit) != 0
        x = jnp.concatenate([jnp.where(upper, other, x), jnp.where(upper, x, other)], axis=0)
        bit *= 2
    return x


def xor_reduce(x, axis, size, combine):
    bit = 1
    while bit < size:
        x = combine(x, lax.ppermute(x, axis, [(i, i ^ bit) for i in range(size)]))
        bit *= 2
    return x


def body(hidden, norm_gain, head_weight, token_ids, lengths, group_ids):
    req_dev, pos_dev, model_width = hidden.shape
    vocab_dev = head_weight.shape[1]
    n_chip = lax.axis_size("chip")
    n_core = lax.axis_size("core")
    n_req = lax.axis_size("req")
    chip = lax.axis_index("chip")
    core = lax.axis_index("core")
    req_index = lax.axis_index("req")
    values = hidden.astype(jnp.float32)
    squares = jnp.mean(values * values, axis=-1, keepdims=True)
    normed = (values * lax.rsqrt(squares + norm_eps) * norm_gain).astype(jnp.bfloat16)
    own_rows = req_dev * pos_dev
    flat_rows = lax.all_gather(normed.reshape(own_rows, model_width), "chip", axis=0, tiled=True)
    other = lax.ppermute(head_weight, "core", [(0, 1), (1, 0)])
    first = core == 0
    weight = jnp.concatenate([jnp.where(first, head_weight, other), jnp.where(first, other, head_weight)], axis=1)
    cols = weight.shape[1]
    weight = jnp.pad(weight, ((0, 0), (0, -cols % 128)))
    weight = lax.optimization_barrier(weight)
    offset = chip * (n_core * vocab_dev)
    half_len = n_chip * pos_dev
    flat_tokens = xor_gather(token_ids, "chip", n_chip, chip).reshape(n_chip * own_rows)
    own_lengths = lax.dynamic_slice_in_dim(lengths, req_index * req_dev, req_dev)
    local_ids = (flat_tokens - offset).reshape(1, -1)
    stats = kernel_stats(flat_rows, weight, local_ids, cols).reshape(4, n_chip, req_dev, pos_dev)
    stats = stats.transpose(0, 2, 1, 3).reshape(4, req_dev, half_len)
    stats = xor_reduce(stats, "chip", n_chip, merge)
    row_top, exp_total, moment, token_logit = stats[0], stats[1], stats[2], stats[3]
    log_total = row_top + jnp.log(exp_total)
    raw_logprob = token_logit - log_total
    raw_entropy = log_total - moment / exp_total
    index = jnp.arange(half_len, dtype=jnp.int32)
    positions = ((index // pos_dev) * n_core + core) * pos_dev + index % pos_dev
    is_live = positions[None, :] < own_lengths[:, None]
    logprob = jnp.where(is_live, raw_logprob, 0.0)
    entropy = jnp.where(is_live, raw_entropy, 0.0)
    half_seq = jnp.sum(logprob, axis=1)
    own_seq = half_seq + lax.ppermute(half_seq, "core", [(0, 1), (1, 0)])
    request_count = lengths.shape[0]
    slots = jnp.arange(request_count, dtype=jnp.int32)
    global_rows = req_index * req_dev + jnp.arange(req_dev, dtype=jnp.int32)
    seq_sum = jnp.sum(jnp.where(slots[None, :] == global_rows[:, None], own_seq[:, None], 0.0), axis=0)
    seq_sum = xor_reduce(seq_sum, "req", n_req, jnp.add)
    same = (group_ids[:, None] == group_ids[None, :]).astype(jnp.float32)
    members = jnp.sum(same, axis=1)
    group_mean = jnp.sum(same * seq_sum[None, :], axis=1) / members
    spread = jnp.sum(same * (seq_sum[None, :] - group_mean[:, None]) ** 2, axis=1) / members
    group_std = jnp.maximum(jnp.sqrt(spread), 1.0)
    centered = (seq_sum - group_mean) / group_std
    own = chip * pos_dev
    return (
        lax.dynamic_slice_in_dim(logprob, own, pos_dev, axis=1),
        lax.dynamic_slice_in_dim(entropy, own, pos_dev, axis=1),
        centered,
    )


def solution(mesh):
    n_req, n_vocab = mesh.devices.shape
    split = Mesh(np.asarray(mesh.devices).reshape(n_req, n_vocab // 2, 2), ("req", "chip", "core"))
    vocab = ("chip", "core")
    return jax.shard_map(
        body,
        mesh=split,
        in_specs=(P("req", vocab, None), P(), P(None, vocab), P("req", vocab), P(), P()),
        out_specs=(P("req", vocab), P("req", vocab), P()),
        check_vma=False,
    )
```

```python
import jax
import jax.numpy as jnp
import numpy as np
from jax import lax
from jax.sharding import Mesh
from jax.sharding import PartitionSpec as P

norm_eps = 1e-06
BLOCK = 3072


def block_stats(rows, tokens, weight, offset):
    logits = jnp.dot(rows, weight, preferred_element_type=jnp.float32)
    row_top = jnp.max(logits, axis=1)
    exps = jnp.exp(logits - row_top[:, None])
    exp_total = jnp.sum(exps, axis=1)
    moment = jnp.sum(exps * logits, axis=1)
    columns = jnp.arange(weight.shape[1], dtype=jnp.int32)
    picked = jnp.sum(jnp.where(columns[None, :] == (tokens - offset)[:, None], logits, 0.0), axis=1)
    return jnp.stack([row_top, exp_total, moment, picked])


def merge(a, b):
    top = jnp.maximum(a[0], b[0])
    ea = jnp.exp(a[0] - top)
    eb = jnp.exp(b[0] - top)
    return jnp.stack([top, a[1] * ea + b[1] * eb, a[2] * ea + b[2] * eb, a[3] + b[3]])


def xor_gather(x, axis, size, index):
    bit = 1
    while bit < size:
        other = lax.ppermute(x, axis, [(i, i ^ bit) for i in range(size)])
        upper = (index & bit) != 0
        x = jnp.concatenate([jnp.where(upper, other, x), jnp.where(upper, x, other)], axis=0)
        bit *= 2
    return x


def xor_reduce(x, axis, size, combine):
    bit = 1
    while bit < size:
        x = combine(x, lax.ppermute(x, axis, [(i, i ^ bit) for i in range(size)]))
        bit *= 2
    return x


def body(hidden, norm_gain, head_weight, token_ids, lengths, group_ids):
    req_dev, pos_dev, model_width = hidden.shape
    vocab_dev = head_weight.shape[1]
    n_chip = lax.axis_size("chip")
    n_core = lax.axis_size("core")
    n_req = lax.axis_size("req")
    chip = lax.axis_index("chip")
    core = lax.axis_index("core")
    req_index = lax.axis_index("req")
    values = hidden.astype(jnp.float32)
    squares = jnp.mean(values * values, axis=-1, keepdims=True)
    normed = (values * lax.rsqrt(squares + norm_eps) * norm_gain).astype(jnp.bfloat16)
    own_rows = req_dev * pos_dev
    flat_rows = lax.all_gather(normed.reshape(own_rows, model_width), "chip", axis=0, tiled=True)
    other = lax.ppermute(head_weight, "core", [(0, 1), (1, 0)])
    first = core == 0
    weight = jnp.concatenate([jnp.where(first, head_weight, other), jnp.where(first, other, head_weight)], axis=1)
    weight = lax.optimization_barrier(weight)
    offset = chip * (n_core * vocab_dev)
    half_len = n_chip * pos_dev
    flat_tokens = xor_gather(token_ids, "chip", n_chip, chip).reshape(n_chip * own_rows)
    own_lengths = lax.dynamic_slice_in_dim(lengths, req_index * req_dev, req_dev)
    blocks = []
    for start in range(0, req_dev * half_len, BLOCK):
        size = min(BLOCK, req_dev * half_len - start)
        blocks.append(block_stats(flat_rows[start : start + size], flat_tokens[start : start + size], weight, offset))
    stats = jnp.concatenate(blocks, axis=1).reshape(4, n_chip, req_dev, pos_dev)
    stats = stats.transpose(0, 2, 1, 3).reshape(4, req_dev, half_len)
    stats = xor_reduce(stats, "chip", n_chip, merge)
    row_top, exp_total, moment, token_logit = stats[0], stats[1], stats[2], stats[3]
    log_total = row_top + jnp.log(exp_total)
    raw_logprob = token_logit - log_total
    raw_entropy = log_total - moment / exp_total
    index = jnp.arange(half_len, dtype=jnp.int32)
    positions = ((index // pos_dev) * n_core + core) * pos_dev + index % pos_dev
    is_live = positions[None, :] < own_lengths[:, None]
    logprob = jnp.where(is_live, raw_logprob, 0.0)
    entropy = jnp.where(is_live, raw_entropy, 0.0)
    half_seq = jnp.sum(logprob, axis=1)
    own_seq = half_seq + lax.ppermute(half_seq, "core", [(0, 1), (1, 0)])
    request_count = lengths.shape[0]
    slots = jnp.arange(request_count, dtype=jnp.int32)
    global_rows = req_index * req_dev + jnp.arange(req_dev, dtype=jnp.int32)
    seq_sum = jnp.sum(jnp.where(slots[None, :] == global_rows[:, None], own_seq[:, None], 0.0), axis=0)
    seq_sum = xor_reduce(seq_sum, "req", n_req, jnp.add)
    same = (group_ids[:, None] == group_ids[None, :]).astype(jnp.float32)
    members = jnp.sum(same, axis=1)
    group_mean = jnp.sum(same * seq_sum[None, :], axis=1) / members
    spread = jnp.sum(same * (seq_sum[None, :] - group_mean[:, None]) ** 2, axis=1) / members
    group_std = jnp.maximum(jnp.sqrt(spread), 1.0)
    centered = (seq_sum - group_mean) / group_std
    own = chip * pos_dev
    return (
        lax.dynamic_slice_in_dim(logprob, own, pos_dev, axis=1),
        lax.dynamic_slice_in_dim(entropy, own, pos_dev, axis=1),
        centered,
    )


def solution(mesh):
    n_req, n_vocab = mesh.devices.shape
    split = Mesh(np.asarray(mesh.devices).reshape(n_req, n_vocab // 2, 2), ("req", "chip", "core"))
    vocab = ("chip", "core")
    return jax.shard_map(
        body,
        mesh=split,
        in_specs=(P("req", vocab, None), P(), P(None, vocab), P("req", vocab), P(), P()),
        out_specs=(P("req", vocab), P("req", vocab), P()),
        check_vma=False,
    )
```

```python
import jax
import jax.numpy as jnp
import numpy as np
from jax import lax
from jax.sharding import Mesh
from jax.sharding import PartitionSpec as P

norm_eps = 1e-06
BLOCK = 1536


def block_stats(rows, tokens, weight, offset):
    logits = jnp.dot(rows, weight, preferred_element_type=jnp.float32)
    row_top = jnp.max(logits, axis=1)
    exps = jnp.exp(logits - row_top[:, None])
    exp_total = jnp.sum(exps, axis=1)
    moment = jnp.sum(exps * logits, axis=1)
    columns = jnp.arange(weight.shape[1], dtype=jnp.int32)
    picked = jnp.sum(jnp.where(columns[None, :] == (tokens - offset)[:, None], logits, 0.0), axis=1)
    return jnp.stack([row_top, exp_total, moment, picked])


def merge(a, b):
    top = jnp.maximum(a[0], b[0])
    ea = jnp.exp(a[0] - top)
    eb = jnp.exp(b[0] - top)
    return jnp.stack([top, a[1] * ea + b[1] * eb, a[2] * ea + b[2] * eb, a[3] + b[3]])


def xor_gather(x, axis, size, index):
    bit = 1
    while bit < size:
        other = lax.ppermute(x, axis, [(i, i ^ bit) for i in range(size)])
        upper = (index & bit) != 0
        x = jnp.concatenate([jnp.where(upper, other, x), jnp.where(upper, x, other)], axis=0)
        bit *= 2
    return x


def xor_reduce(x, axis, size, combine):
    bit = 1
    while bit < size:
        x = combine(x, lax.ppermute(x, axis, [(i, i ^ bit) for i in range(size)]))
        bit *= 2
    return x


def body(hidden, norm_gain, head_weight, token_ids, lengths, group_ids):
    req_dev, pos_dev, model_width = hidden.shape
    vocab_dev = head_weight.shape[1]
    n_chip = lax.axis_size("chip")
    n_core = lax.axis_size("core")
    n_req = lax.axis_size("req")
    chip = lax.axis_index("chip")
    core = lax.axis_index("core")
    req_index = lax.axis_index("req")
    values = hidden.astype(jnp.float32)
    squares = jnp.mean(values * values, axis=-1, keepdims=True)
    normed = (values * lax.rsqrt(squares + norm_eps) * norm_gain).astype(jnp.bfloat16)
    own_rows = req_dev * pos_dev
    flat_rows = lax.all_gather(normed.reshape(own_rows, model_width), "chip", axis=0, tiled=True)
    other = lax.ppermute(head_weight, "core", [(0, 1), (1, 0)])
    first = core == 0
    weight = jnp.concatenate([jnp.where(first, head_weight, other), jnp.where(first, other, head_weight)], axis=1)
    weight = lax.optimization_barrier(weight)
    offset = chip * (n_core * vocab_dev)
    half_len = n_chip * pos_dev
    flat_tokens = xor_gather(token_ids, "chip", n_chip, chip).reshape(n_chip * own_rows)
    own_lengths = lax.dynamic_slice_in_dim(lengths, req_index * req_dev, req_dev)
    blocks = []
    for start in range(0, req_dev * half_len, BLOCK):
        size = min(BLOCK, req_dev * half_len - start)
        part = block_stats(flat_rows[start : start + size], flat_tokens[start : start + size], weight, offset)
        blocks.append(xor_reduce(part, "chip", n_chip, merge))
    stats = jnp.concatenate(blocks, axis=1).reshape(4, n_chip, req_dev, pos_dev)
    stats = stats.transpose(0, 2, 1, 3).reshape(4, req_dev, half_len)
    row_top, exp_total, moment, token_logit = stats[0], stats[1], stats[2], stats[3]
    log_total = row_top + jnp.log(exp_total)
    raw_logprob = token_logit - log_total
    raw_entropy = log_total - moment / exp_total
    index = jnp.arange(half_len, dtype=jnp.int32)
    positions = ((index // pos_dev) * n_core + core) * pos_dev + index % pos_dev
    is_live = positions[None, :] < own_lengths[:, None]
    logprob = jnp.where(is_live, raw_logprob, 0.0)
    entropy = jnp.where(is_live, raw_entropy, 0.0)
    half_seq = jnp.sum(logprob, axis=1)
    own_seq = half_seq + lax.ppermute(half_seq, "core", [(0, 1), (1, 0)])
    request_count = lengths.shape[0]
    slots = jnp.arange(request_count, dtype=jnp.int32)
    global_rows = req_index * req_dev + jnp.arange(req_dev, dtype=jnp.int32)
    seq_sum = jnp.sum(jnp.where(slots[None, :] == global_rows[:, None], own_seq[:, None], 0.0), axis=0)
    seq_sum = xor_reduce(seq_sum, "req", n_req, jnp.add)
    same = (group_ids[:, None] == group_ids[None, :]).astype(jnp.float32)
    members = jnp.sum(same, axis=1)
    group_mean = jnp.sum(same * seq_sum[None, :], axis=1) / members
    spread = jnp.sum(same * (seq_sum[None, :] - group_mean[:, None]) ** 2, axis=1) / members
    group_std = jnp.maximum(jnp.sqrt(spread), 1.0)
    centered = (seq_sum - group_mean) / group_std
    own = chip * pos_dev
    return (
        lax.dynamic_slice_in_dim(logprob, own, pos_dev, axis=1),
        lax.dynamic_slice_in_dim(entropy, own, pos_dev, axis=1),
        centered,
    )


def solution(mesh):
    n_req, n_vocab = mesh.devices.shape
    split = Mesh(np.asarray(mesh.devices).reshape(n_req, n_vocab // 2, 2), ("req", "chip", "core"))
    vocab = ("chip", "core")
    return jax.shard_map(
        body,
        mesh=split,
        in_specs=(P("req", vocab, None), P(), P(None, vocab), P("req", vocab), P(), P()),
        out_specs=(P("req", vocab), P("req", vocab), P()),
        check_vma=False,
    )
```
